32 devices in a mesh: ctx: 16 (over z, y, x), head: 2 (over core).
Axes of the slice: x: 2, y: 2, z: 4, core: 2. Of those that a mesh axis runs over, the one named last changes fastest.
Arguments:
- queries: bfloat16 [2048, 4096], P('ctx', 'head'), may hold values from -48 to 48
- keys: bfloat16 [2048, 2048], P('ctx', 'head'), may hold values from -6 to 6
- values: bfloat16 [2048, 2048], P('ctx', 'head'), may hold values from -6 to 6
- hidden_in: bfloat16 [2048, 4608], P('ctx', 'head'), may hold values from -6 to 6
- out_weight: bfloat16 [4096, 4608], P('ctx', 'head'), may hold values from -0.09375 to 0.09375
- out_gain: float32 [4608], P('head'), may hold values from 0.1 to 1.9
- reward_weight: float32 [4608], P('head'), may hold values from -0.09375 to 0.09375
- doc_lengths: int32 [16], replicated, may hold values from 1 to 1024, 2048 in all
Outputs:
- hidden_out: bfloat16 [2048, 4608], P('ctx', 'head')
- rewards: float32 [16], replicated
The draws below stay inside these ranges and needn't reach their ends.
Inputs may be any that keep to these rules, and one draw needn't show every extreme that they name: `doc_lengths`: the lengths sum to 2048; the longest is exactly 1024.
All inputs are finite; a program needn't handle non-finite values.
Results may differ from the reference program's by a relative error of at most 0.005.
Values may be sent and summed in bfloat16 or wider, within the bound.
No kernel may reach another device: no remote copies, remote signals or barrier semaphores. Data moves between devices by JAX's collectives and lax.ppermute only.
A program may use at most 128 MiB of HBM per device.

```python
import math
import jax
import jax.numpy as jnp
import numpy as np
from jax import lax

D = 4608
QUERY_HEADS = 32
KEY_VALUE_HEADS = 16
HEAD_WIDTH = 128
TOK_DEV = 128
NDOC = 16
PACK_TOKENS = 2048
DOC_MAX = 1024
N_CTX = 16


def draw_queries(key, part):
    first_key, second_key = jax.random.split(key)
    base = jax.random.truncated_normal(first_key, -4.0, 4.0, (PACK_TOKENS, QUERY_HEADS, HEAD_WIDTH), jnp.float32)
    lowest = 1.0
    exponent = jax.random.uniform(second_key, (PACK_TOKENS, QUERY_HEADS, 1), jnp.float32, math.log(lowest), math.log(12.0))
    factor = jnp.exp(exponent)
    return (base * factor).reshape(PACK_TOKENS, QUERY_HEADS * HEAD_WIDTH).astype(jnp.bfloat16)


def block_levels(own_key, shape, pieces, smallest, high):
    def one(position, blocks):
        heights = jax.random.uniform(jax.random.fold_in(jax.random.fold_in(own_key, 6), position), (blocks,), jnp.float32, smallest / len(pieces), high / len(pieces))
        return jnp.repeat(jnp.exp(heights), shape[position] // blocks).reshape((-1,) + (1,) * (len(shape) - position - 1))

    factor_of = one(*pieces[0])
    for cut in pieces[1:]:
        factor_of = factor_of * one(*cut)
    return factor_of


def length_profile(amount, total, limit, lean):
    weights = [(1 << 20) // math.isqrt(grade ** lean) + 1 for grade in range(2, amount + 1)]
    surplus, holding = total - limit - (amount - 1), [1] * (amount - 1)
    while surplus > 0:
        movable = [i for i in range(amount - 1) if holding[i] < limit]
        whole, left = sum([weights[i] for i in movable]), surplus
        for i in movable:
            extra = min(limit - holding[i], max(1, left * weights[i] // whole), surplus)
            holding[i] = holding[i] + extra
            surplus = surplus - extra
    return np.array([limit] + holding)


def ragged_sizes(rng, count, total, reach, slope):
    if count == 2:
        one = jax.random.randint(rng, (), max(1, total - reach), min(reach, total - 1) + 1)
        return jnp.stack([one, total - one])
    sizes = jnp.asarray(length_profile(count, total, reach, slope), jnp.int32)
    couples = (count - 1) // 2
    giver, receiver = sizes[1:1 + 2 * couples:2], sizes[2:2 + 2 * couples:2]
    margin = jnp.minimum(giver - 1, reach - receiver)
    passed = jax.random.randint(jax.random.fold_in(rng, 1), (couples,), 0, 1 << 20) % (margin + 1)
    sizes = sizes.at[1:1 + 2 * couples:2].set(giver - passed).at[2:2 + 2 * couples:2].set(receiver + passed)
    return sizes[jax.random.permutation(jax.random.fold_in(rng, 2), count)]


def scatter_about(own_key, shape, deviation, most, cuts=(), kind=jnp.bfloat16):
    values = jax.random.normal(own_key, shape, jnp.float32) * deviation
    if len(cuts) > 0:
        values = block_levels(own_key, shape, cuts, -0.22, 0.18) * values
    return jnp.clip(values, min=-most, max=most).astype(kind)


def setup_inputs(seed: int = 0) -> dict:
    streams_of = jax.random.split(jax.random.key(seed), 9)
    return {
        "queries": draw_queries(jax.random.fold_in(streams_of[8], 71), 0),
        "keys": scatter_about(streams_of[1], (PACK_TOKENS, KEY_VALUE_HEADS * HEAD_WIDTH), 1.0, 6.0, ((0, 16), (1, 2))),
        "values": scatter_about(streams_of[2], (PACK_TOKENS, KEY_VALUE_HEADS * HEAD_WIDTH), 1.0, 6.0, ((0, 16), (1, 2))),
        "hidden_in": scatter_about(streams_of[3], (PACK_TOKENS, D), 1.0, 6.0, ((0, 16), (1, 2))),
        "out_weight": scatter_about(streams_of[4], (QUERY_HEADS * HEAD_WIDTH, D), (QUERY_HEADS * HEAD_WIDTH) ** -0.5, 0.09375, ((0, 16), (1, 2))),
        "out_gain": jnp.clip(1.0 + 0.18 * jax.random.normal(streams_of[5], (D,), jnp.float32), 0.1, 1.9),
        "reward_weight": scatter_about(streams_of[6], (D,), D ** -0.5, 0.09375, ((0, 2),), jnp.float32),
        "doc_lengths": ragged_sizes(streams_of[7], NDOC, PACK_TOKENS, DOC_MAX, 2).astype(jnp.int32),
    }


soft_cap = 50.0

def storage_positions(rows):
    owner = rows // TOK_DEV
    offset = rows % TOK_DEV
    half = TOK_DEV // 2
    slab = jnp.where(offset < half, owner, 2 * N_CTX - 1 - owner)
    return (slab * half + offset % half).astype(jnp.int32)

def reference(queries, keys, values, hidden_in, out_weight, out_gain, reward_weight, doc_lengths):
    rows = jnp.arange(PACK_TOKENS, dtype=jnp.int32)
    positions = storage_positions(rows)
    doc_ends = jnp.cumsum(doc_lengths).astype(jnp.int32)
    doc_ids = lax.optimization_barrier(jnp.sum((positions[:, None] >= doc_ends[None, :]).astype(jnp.int32), axis=1))
    group_repeat = QUERY_HEADS // KEY_VALUE_HEADS
    scale = (D / QUERY_HEADS) ** (-0.5)
    query_head_rows = queries.reshape(PACK_TOKENS, KEY_VALUE_HEADS, group_repeat, HEAD_WIDTH).transpose(1, 0, 2, 3)
    key_head_rows = keys.reshape(PACK_TOKENS, KEY_VALUE_HEADS, HEAD_WIDTH).transpose(1, 0, 2)
    value_head_rows = values.reshape(PACK_TOKENS, KEY_VALUE_HEADS, HEAD_WIDTH).transpose(1, 0, 2)
    block = min(512, PACK_TOKENS)
    nblocks = PACK_TOKENS // block

    def head_fn(operands):
        q_one, k_one, v_one = operands
        k_float = k_one.astype(jnp.float32)
        v_float = v_one.astype(jnp.float32)

        def block_fn(index):
            first = (index * block).astype(jnp.int32)
            q_block = lax.dynamic_slice_in_dim(q_one, first, block, 0).astype(jnp.float32)
            q_pos = lax.dynamic_slice_in_dim(positions, first, block, 0)
            q_doc = lax.dynamic_slice_in_dim(doc_ids, first, block, 0)
            scores = jnp.einsum('qrd,kd->rqk', q_block, k_float) * scale
            scores = soft_cap * jnp.tanh(scores / soft_cap)
            visible = (q_doc[:, None] == doc_ids[None, :]) & (positions[None, :] <= q_pos[:, None])
            weights = jnp.where(visible[None], jnp.exp(scores), 0.0)
            denominator = lax.optimization_barrier(jnp.sum(weights, axis=-1))
            rounded = weights.astype(jnp.bfloat16).astype(jnp.float32)
            numerator = jnp.einsum('rqk,kd->rqd', rounded, v_float)
            return (numerator / denominator[..., None]).astype(jnp.bfloat16)
        result = lax.map(block_fn, jnp.arange(nblocks, dtype=jnp.int32))
        return result.transpose(0, 2, 1, 3).reshape(PACK_TOKENS, group_repeat, HEAD_WIDTH)
    attended = lax.map(head_fn, (query_head_rows, key_head_rows, value_head_rows))
    attended = attended.transpose(1, 0, 2, 3).reshape(PACK_TOKENS, QUERY_HEADS * HEAD_WIDTH)
    mixed = jnp.dot(attended, out_weight, preferred_element_type=jnp.float32)
    squares = lax.optimization_barrier(jnp.sum(mixed * mixed, axis=1))
    normed = mixed / jnp.sqrt(squares / D + 1e-06)[:, None]
    out32 = hidden_in.astype(jnp.float32) + normed * out_gain[None, :]
    tok_reward = lax.optimization_barrier(jnp.sum(out32 * reward_weight[None, :], axis=1))
    onehot = (doc_ids[:, None] == jnp.arange(NDOC, dtype=jnp.int32)[None, :]).astype(jnp.float32)
    sums = lax.optimization_barrier(jnp.sum(onehot * tok_reward[:, None], axis=0))
    rewards = sums / jnp.sqrt(doc_lengths.astype(jnp.float32))
    return (out32.astype(jnp.bfloat16), rewards)
```

```python
import jax
import jax.numpy as jnp
from jax import lax
from jax.sharding import Mesh, PartitionSpec as P

D = 4608
QUERY_HEADS = 32
KEY_VALUE_HEADS = 16
HEAD_WIDTH = 128
NDOC = 16


soft_cap = 50.0
CTX = ("ca", "cb")


def storage_positions(rows, tok_dev, n_ctx):
    owner = rows // tok_dev
    offset = rows % tok_dev
    half = tok_dev // 2
    slab = jnp.where(offset < half, owner, 2 * n_ctx - 1 - owner)
    return slab * half + offset % half


def document_of(positions, doc_ends):
    return jnp.sum((positions[:, None] >= doc_ends[None, :]).astype(jnp.int32), axis=1)


def shards(queries, keys, values, hidden_in, out_weight, out_gain, reward_weight, doc_lengths):
    n_ctx = lax.axis_size(CTX)
    device = lax.axis_index(CTX)
    tok_dev = queries.shape[0]
    kv_local = keys.shape[1] // HEAD_WIDTH
    group_repeat = QUERY_HEADS // KEY_VALUE_HEADS
    scale = (D / QUERY_HEADS) ** (-0.5)
    doc_ends = jnp.cumsum(doc_lengths)
    local_rows = device * tok_dev + jnp.arange(tok_dev, dtype=jnp.int32)
    query_pos = storage_positions(local_rows, tok_dev, n_ctx)
    query_doc = document_of(query_pos, doc_ends)
    q_groups = queries.reshape(tok_dev, kv_local, group_repeat, HEAD_WIDTH)
    span = tok_dev * max(1, 2048 // tok_dev)

    def attend_block(state, key_piece, value_piece, start):
        count = key_piece.shape[0]
        key_rows = start + jnp.arange(count, dtype=jnp.int32)
        key_pos = storage_positions(key_rows, tok_dev, n_ctx)
        key_doc = document_of(key_pos, doc_ends)
        visible = (query_doc[:, None] == key_doc[None, :]) & (
            key_pos[None, :] <= query_pos[:, None]
        )

        def compute(carry):
            numerator, denominator = carry
            scores = (
                jnp.einsum(
                    "qgrd,kgd->grqk",
                    q_groups,
                    key_piece.reshape(count, kv_local, HEAD_WIDTH),
                    preferred_element_type=jnp.float32,
                )
                * scale
            )
            scores = soft_cap * jnp.tanh(scores / soft_cap)
            weights = jnp.where(visible[None, None], jnp.exp(scores), 0.0)
            numerator = numerator + jnp.einsum(
                "grqk,kgd->grqd",
                weights.astype(jnp.bfloat16),
                value_piece.reshape(count, kv_local, HEAD_WIDTH),
                preferred_element_type=jnp.float32,
            )
            denominator = denominator + jnp.sum(weights, axis=-1)
            return (numerator, denominator)

        return lax.cond(jnp.any(visible), compute, lambda carry: carry, state)

    def attend(state, key_piece, value_piece, start):
        count = key_piece.shape[0]
        if count <= span:
            return attend_block(state, key_piece, value_piece, start)
        blocks = count // span
        whole = blocks * span
        width = key_piece.shape[1]
        key_blocks = key_piece[:whole].reshape(blocks, span, width)
        value_blocks = value_piece[:whole].reshape(blocks, span, width)
        starts = start + span * jnp.arange(blocks, dtype=jnp.int32)

        def step_fn(carry, item):
            return (attend_block(carry, item[0], item[1], item[2]), None)

        state, _ = lax.scan(step_fn, state, (key_blocks, value_blocks, starts))
        if whole < count:
            state = attend_block(state, key_piece[whole:], value_piece[whole:], start + whole)
        return state

    initial = (
        jnp.zeros((kv_local, group_repeat, tok_dev, HEAD_WIDTH), jnp.float32),
        jnp.zeros((kv_local, group_repeat, tok_dev), jnp.float32),
    )
    kv_width = keys.shape[1]
    both = lax.all_gather(jnp.concatenate([keys, values], axis=1), CTX, axis=0, tiled=True)
    numerator, denominator = attend(initial, both[:, :kv_width], both[:, kv_width:], jnp.int32(0))
    attended = (numerator / denominator[..., None]).astype(jnp.bfloat16)
    attended = attended.transpose(2, 0, 1, 3).reshape(tok_dev, kv_local * group_repeat * HEAD_WIDTH)
    all_heads = lax.all_gather(attended, "head", axis=1, tiled=True)
    weight_rows = lax.all_gather(out_weight, "cb", axis=0, tiled=True)
    regrouped = lax.all_to_all(all_heads, "ca", 1, 0, tiled=True)
    partial = jnp.dot(regrouped, weight_rows, preferred_element_type=jnp.float32)
    mixed = lax.psum_scatter(partial, "ca", scatter_dimension=0, tiled=True)
    squares = lax.psum(jnp.sum(mixed * mixed, axis=1), "head")
    normed = mixed / jnp.sqrt(squares / D + 1e-06)[:, None]
    out32 = hidden_in.astype(jnp.float32) + normed * out_gain[None, :]
    tok_reward = jnp.sum(out32 * reward_weight[None, :], axis=1)
    onehot = (query_doc[:, None] == jnp.arange(NDOC, dtype=jnp.int32)[None, :]).astype(jnp.float32)
    partial_sums = jnp.sum(onehot * tok_reward[:, None], axis=0)
    totals = lax.psum(partial_sums, CTX + ("head",))
    rewards = totals / jnp.sqrt(doc_lengths.astype(jnp.float32))
    return (out32.astype(jnp.bfloat16), rewards)


def solution(mesh):
    n_ctx, n_head = mesh.devices.shape
    inner = 1
    while inner * inner * 4 <= n_ctx:
        inner *= 2
    split = Mesh(mesh.devices.reshape(n_ctx // inner, inner, n_head), ("ca", "cb", "head"))
    rows = P(CTX, "head")
    in_specs = (rows, rows, rows, rows, rows, P("head"), P("head"), P())
    out_specs = (rows, P())
    return jax.shard_map(shards, mesh=split, in_specs=in_specs, out_specs=out_specs, check_vma=False)
```

```python
import jax
import jax.numpy as jnp
from jax import lax
from jax.sharding import Mesh, PartitionSpec as P

D = 4608
QUERY_HEADS = 32
KEY_VALUE_HEADS = 16
HEAD_WIDTH = 128
NDOC = 16


soft_cap = 50.0
CTX = ("ca", "cb")


def storage_positions(rows, tok_dev, n_ctx):
    owner = rows // tok_dev
    offset = rows % tok_dev
    half = tok_dev // 2
    slab = jnp.where(offset < half, owner, 2 * n_ctx - 1 - owner)
    return slab * half + offset % half


def document_of(positions, doc_ends):
    return jnp.sum((positions[:, None] >= doc_ends[None, :]).astype(jnp.int32), axis=1)


def shards(queries, keys, values, hidden_in, out_weight, out_gain, reward_weight, doc_lengths):
    n_ctx = lax.axis_size(CTX)
    device = lax.axis_index(CTX)
    tok_dev = queries.shape[0]
    kv_local = keys.shape[1] // HEAD_WIDTH
    group_repeat = QUERY_HEADS // KEY_VALUE_HEADS
    scale = (D / QUERY_HEADS) ** (-0.5)
    doc_ends = jnp.cumsum(doc_lengths)
    local_rows = device * tok_dev + jnp.arange(tok_dev, dtype=jnp.int32)
    query_pos = storage_positions(local_rows, tok_dev, n_ctx)
    query_doc = document_of(query_pos, doc_ends)
    q_groups = queries.reshape(tok_dev, kv_local, group_repeat, HEAD_WIDTH)
    span = tok_dev * max(1, 2048 // tok_dev)

    def attend_block(state, key_piece, value_piece, start):
        count = key_piece.shape[0]
        key_rows = start + jnp.arange(count, dtype=jnp.int32)
        key_pos = storage_positions(key_rows, tok_dev, n_ctx)
        key_doc = document_of(key_pos, doc_ends)
        visible = (query_doc[:, None] == key_doc[None, :]) & (
            key_pos[None, :] <= query_pos[:, None]
        )

        def compute(carry):
            numerator, denominator = carry
            scores = (
                jnp.einsum(
                    "qgrd,kgd->grqk",
                    q_groups,
                    key_piece.reshape(count, kv_local, HEAD_WIDTH),
                    preferred_element_type=jnp.float32,
                )
                * scale
            )
            scores = soft_cap * jnp.tanh(scores / soft_cap)
            weights = jnp.where(visible[None, None], jnp.exp(scores), 0.0)
            numerator = numerator + jnp.einsum(
                "grqk,kgd->grqd",
                weights.astype(jnp.bfloat16),
                value_piece.reshape(count, kv_local, HEAD_WIDTH),
                preferred_element_type=jnp.float32,
            )
            denominator = denominator + jnp.sum(weights, axis=-1)
            return (numerator, denominator)

        return lax.cond(jnp.any(visible), compute, lambda carry: carry, state)

    def attend(state, key_piece, value_piece, start):
        count = key_piece.shape[0]
        if count <= span:
            return attend_block(state, key_piece, value_piece, start)
        blocks = count // span
        whole = blocks * span
        width = key_piece.shape[1]
        key_blocks = key_piece[:whole].reshape(blocks, span, width)
        value_blocks = value_piece[:whole].reshape(blocks, span, width)
        starts = start + span * jnp.arange(blocks, dtype=jnp.int32)

        def step_fn(carry, item):
            return (attend_block(carry, item[0], item[1], item[2]), None)

        state, _ = lax.scan(step_fn, state, (key_blocks, value_blocks, starts))
        if whole < count:
            state = attend_block(state, key_piece[whole:], value_piece[whole:], start + whole)
        return state

    initial = (
        jnp.zeros((kv_local, group_repeat, tok_dev, HEAD_WIDTH), jnp.float32),
        jnp.zeros((kv_local, group_repeat, tok_dev), jnp.float32),
    )
    outer = lax.axis_size("ca")
    inner = lax.axis_size("cb")
    rows_each = out_weight.shape[0]
    place = lax.axis_index("ca")
    pieces = [out_weight] + [
        lax.ppermute(out_weight, "ca", [(i, (i - shift) % outer) for i in range(outer)])
        for shift in range(1, outer)
    ]
    kv_width = keys.shape[1]
    both = lax.all_gather(jnp.concatenate([keys, values], axis=1), CTX, axis=0, tiled=True)
    both, pieces = lax.optimization_barrier((both, pieces))
    numerator, denominator = attend(initial, both[:, :kv_width], both[:, kv_width:], jnp.int32(0))
    attended = (numerator / denominator[..., None]).astype(jnp.bfloat16)
    attended = attended.transpose(2, 0, 1, 3).reshape(tok_dev, kv_local * group_repeat * HEAD_WIDTH)
    all_heads = lax.all_gather(attended, "head", axis=1, tiled=True)
    weight_rows = jnp.stack(pieces).reshape(outer * rows_each, out_weight.shape[1])
    blocks = all_heads.reshape(tok_dev, outer, inner, rows_each).transpose(2, 0, 1, 3)
    regrouped = lax.all_to_all(blocks, "cb", 0, 0, tiled=True)
    regrouped = jnp.roll(regrouped.reshape(inner * tok_dev, outer, rows_each), -place, axis=1)
    partial = jnp.dot(
        regrouped.reshape(inner * tok_dev, outer * rows_each), weight_rows, preferred_element_type=jnp.float32
    )
    mixed = lax.psum_scatter(partial, "cb", scatter_dimension=0, tiled=True)
    squares = lax.psum(jnp.sum(mixed * mixed, axis=1), "head")
    normed = mixed / jnp.sqrt(squares / D + 1e-06)[:, None]
    out32 = hidden_in.astype(jnp.float32) + normed * out_gain[None, :]
    tok_reward = jnp.sum(out32 * reward_weight[None, :], axis=1)
    onehot = (query_doc[:, None] == jnp.arange(NDOC, dtype=jnp.int32)[None, :]).astype(jnp.float32)
    partial_sums = jnp.sum(onehot * tok_reward[:, None], axis=0)
    totals = lax.psum(partial_sums, CTX + ("head",))
    rewards = totals / jnp.sqrt(doc_lengths.astype(jnp.float32))
    return (out32.astype(jnp.bfloat16), rewards)


def solution(mesh):
    n_ctx, n_head = mesh.devices.shape
    inner = 1
    while inner * inner * 4 <= n_ctx:
        inner *= 2
    split = Mesh(mesh.devices.reshape(n_ctx // inner, inner, n_head), ("ca", "cb", "head"))
    rows = P(CTX, "head")
    in_specs = (rows, rows, rows, rows, rows, P("head"), P("head"), P())
    out_specs = (rows, P())
    return jax.shard_map(shards, mesh=split, in_specs=in_specs, out_specs=out_specs, check_vma=False)
```

```python
import jax
import jax.numpy as jnp
from jax import lax
from jax.sharding import Mesh, PartitionSpec as P

D = 4608
QUERY_HEADS = 32
KEY_VALUE_HEADS = 16
HEAD_WIDTH = 128
NDOC = 16


soft_cap = 50.0
CTX = ("ca", "cb")


def storage_positions(rows, tok_dev, n_ctx):
    owner = rows // tok_dev
    offset = rows % tok_dev
    half = tok_dev // 2
    slab = jnp.where(offset < half, owner, 2 * n_ctx - 1 - owner)
    return slab * half + offset % half


def document_of(positions, doc_ends):
    return jnp.sum((positions[:, None] >= doc_ends[None, :]).astype(jnp.int32), axis=1)


def butterfly_sum(x, axes):
    for axis in axes:
        size = lax.axis_size(axis)
        bit = 1
        while bit < size:
            x = x + lax.ppermute(x, axis, [(i, i ^ bit) for i in range(size)])
            bit *= 2
    return x


def shards(queries, keys, values, hidden_in, out_weight, out_gain, reward_weight, doc_lengths):
    n_ctx = lax.axis_size(CTX)
    device = lax.axis_index(CTX)
    tok_dev = queries.shape[0]
    kv_local = keys.shape[1] // HEAD_WIDTH
    group_repeat = QUERY_HEADS // KEY_VALUE_HEADS
    scale = (D / QUERY_HEADS) ** (-0.5)
    doc_ends = jnp.cumsum(doc_lengths)
    local_rows = device * tok_dev + jnp.arange(tok_dev, dtype=jnp.int32)
    query_pos = storage_positions(local_rows, tok_dev, n_ctx)
    query_doc = document_of(query_pos, doc_ends)
    q_groups = queries.reshape(tok_dev, kv_local, group_repeat, HEAD_WIDTH)
    span = tok_dev * max(1, 2048 // tok_dev)

    def attend_block(state, key_piece, value_piece, start):
        count = key_piece.shape[0]
        key_rows = start + jnp.arange(count, dtype=jnp.int32)
        key_pos = storage_positions(key_rows, tok_dev, n_ctx)
        key_doc = document_of(key_pos, doc_ends)
        visible = (query_doc[:, None] == key_doc[None, :]) & (
            key_pos[None, :] <= query_pos[:, None]
        )

        def compute(carry):
            numerator, denominator = carry
            scores = (
                jnp.einsum(
                    "qgrd,kgd->grqk",
                    q_groups,
                    key_piece.reshape(count, kv_local, HEAD_WIDTH),
                    preferred_element_type=jnp.float32,
                )
                * scale
            )
            scores = soft_cap * jnp.tanh(scores / soft_cap)
            weights = jnp.where(visible[None, None], jnp.exp(scores), 0.0)
            numerator = numerator + jnp.einsum(
                "grqk,kgd->grqd",
                weights.astype(jnp.bfloat16),
                value_piece.reshape(count, kv_local, HEAD_WIDTH),
                preferred_element_type=jnp.float32,
            )
            denominator = denominator + jnp.sum(weights, axis=-1)
            return (numerator, denominator)

        return lax.cond(jnp.any(visible), compute, lambda carry: carry, state)

    def attend(state, key_piece, value_piece, start):
        count = key_piece.shape[0]
        if count <= span:
            return attend_block(state, key_piece, value_piece, start)
        blocks = count // span
        whole = blocks * span
        width = key_piece.shape[1]
        key_blocks = key_piece[:whole].reshape(blocks, span, width)
        value_blocks = value_piece[:whole].reshape(blocks, span, width)
        starts = start + span * jnp.arange(blocks, dtype=jnp.int32)

        def step_fn(carry, item):
            return (attend_block(carry, item[0], item[1], item[2]), None)

        state, _ = lax.scan(step_fn, state, (key_blocks, value_blocks, starts))
        if whole < count:
            state = attend_block(state, key_piece[whole:], value_piece[whole:], start + whole)
        return state

    initial = (
        jnp.zeros((kv_local, group_repeat, tok_dev, HEAD_WIDTH), jnp.float32),
        jnp.zeros((kv_local, group_repeat, tok_dev), jnp.float32),
    )
    outer = lax.axis_size("ca")
    inner = lax.axis_size("cb")
    rows_each = out_weight.shape[0]
    place = lax.axis_index("ca")
    pieces = [out_weight] + [
        lax.ppermute(out_weight, "ca", [(i, (i - shift) % outer) for i in range(outer)])
        for shift in range(1, outer)
    ]
    kv_width = keys.shape[1]
    both = lax.all_gather(jnp.concatenate([keys, values], axis=1), CTX, axis=0, tiled=True)
    both, pieces = lax.optimization_barrier((both, pieces))
    numerator, denominator = attend(initial, both[:, :kv_width], both[:, kv_width:], jnp.int32(0))
    attended = (numerator / denominator[..., None]).astype(jnp.bfloat16)
    attended = attended.transpose(2, 0, 1, 3).reshape(tok_dev, kv_local * group_repeat * HEAD_WIDTH)
    all_heads = lax.all_gather(attended, "head", axis=1, tiled=True)
    weight_rows = jnp.stack(pieces).reshape(outer * rows_each, out_weight.shape[1])
    blocks = all_heads.reshape(tok_dev, outer, inner, rows_each).transpose(2, 0, 1, 3)
    regrouped = lax.all_to_all(blocks, "cb", 0, 0, tiled=True)
    regrouped = jnp.roll(regrouped.reshape(inner * tok_dev, outer, rows_each), -place, axis=1)
    partial = jnp.dot(
        regrouped.reshape(inner * tok_dev, outer * rows_each), weight_rows, preferred_element_type=jnp.float32
    )
    mixed = lax.psum_scatter(partial, "cb", scatter_dimension=0, tiled=True)
    squares = lax.psum(jnp.sum(mixed * mixed, axis=1), "head")
    normed = mixed / jnp.sqrt(squares / D + 1e-06)[:, None]
    out32 = hidden_in.astype(jnp.float32) + normed * out_gain[None, :]
    tok_reward = jnp.sum(out32 * reward_weight[None, :], axis=1)
    onehot = (query_doc[:, None] == jnp.arange(NDOC, dtype=jnp.int32)[None, :]).astype(jnp.float32)
    partial_sums = jnp.sum(onehot * tok_reward[:, None], axis=0)
    totals = butterfly_sum(partial_sums, CTX + ("head",))
    rewards = totals / jnp.sqrt(doc_lengths.astype(jnp.float32))
    return (out32.astype(jnp.bfloat16), rewards)


def solution(mesh):
    n_ctx, n_head = mesh.devices.shape
    inner = 1
    while inner * inner * 4 <= n_ctx:
        inner *= 2
    split = Mesh(mesh.devices.reshape(n_ctx // inner, inner, n_head), ("ca", "cb", "head"))
    rows = P(CTX, "head")
    in_specs = (rows, rows, rows, rows, rows, P("head"), P("head"), P())
    out_specs = (rows, P())
    return jax.shard_map(shards, mesh=split, in_specs=in_specs, out_specs=out_specs, check_vma=False)
```

```python
import jax
import jax.numpy as jnp
from jax import lax
from jax.sharding import Mesh, PartitionSpec as P

D = 4608
QUERY_HEADS = 32
KEY_VALUE_HEADS = 16
HEAD_WIDTH = 128
NDOC = 16


soft_cap = 50.0
CTX = ("c0", "c1", "c2")
INNER = ("c1", "c2")


def storage_positions(rows, tok_dev, n_ctx):
    owner = rows // tok_dev
    offset = rows % tok_dev
    half = tok_dev // 2
    slab = jnp.where(offset < half, owner, 2 * n_ctx - 1 - owner)
    return slab * half + offset % half


def document_of(positions, doc_ends):
    return jnp.sum((positions[:, None] >= doc_ends[None, :]).astype(jnp.int32), axis=1)


def line_gather(x, axis):
    n = lax.axis_size(axis)
    i = lax.axis_index(axis)
    if n == 2:
        other = lax.ppermute(x, axis, [(0, 1), (1, 0)])
        return lax.dynamic_slice_in_dim(jnp.stack([x, other, x]), i, 2, axis=0)
    ahead, behind = x, x
    from_left, from_right = [], []
    for _ in range(n - 1):
        ahead = lax.ppermute(ahead, axis, [(k, k + 1) for k in range(n - 1)])
        behind = lax.ppermute(behind, axis, [(k + 1, k) for k in range(n - 1)])
        from_left.append(ahead)
        from_right.append(behind)
    stacked = jnp.stack(from_left[::-1] + [x] + from_right)
    return lax.dynamic_slice_in_dim(stacked, (n - 1) - i, n, axis=0)


def gather_tokens(x):
    width = x.shape[1]
    first = (width // 4) // 128 * 128
    second = first + (width - first) // 2 // 128 * 128
    part_a, part_b, part_c = x[:, :first], x[:, first:second], x[:, second:]
    got_a = line_gather(line_gather(line_gather(part_a, "c2"), "c1"), "c0")
    got_b = line_gather(line_gather(line_gather(part_b, "c0"), "c2"), "c1").transpose(2, 0, 1, 3, 4)
    got_c = line_gather(line_gather(line_gather(part_c, "c0"), "c1"), "c2").transpose(2, 1, 0, 3, 4)
    rows = lax.axis_size(CTX) * x.shape[0]
    return jnp.concatenate([g.reshape(rows, -1) for g in (got_a, got_b, got_c)], axis=1)


def butterfly_sum(x, axes):
    for axis in axes:
        size = lax.axis_size(axis)
        bit = 1
        while bit < size:
            x = x + lax.ppermute(x, axis, [(i, i ^ bit) for i in range(size)])
            bit *= 2
    return x


def shards(queries, keys, values, hidden_in, out_weight, out_gain, reward_weight, doc_lengths):
    n_ctx = lax.axis_size(CTX)
    device = lax.axis_index(CTX)
    tok_dev = queries.shape[0]
    kv_local = keys.shape[1] // HEAD_WIDTH
    group_repeat = QUERY_HEADS // KEY_VALUE_HEADS
    scale = (D / QUERY_HEADS) ** (-0.5)
    doc_ends = jnp.cumsum(doc_lengths)
    local_rows = device * tok_dev + jnp.arange(tok_dev, dtype=jnp.int32)
    query_pos = storage_positions(local_rows, tok_dev, n_ctx)
    query_doc = document_of(query_pos, doc_ends)
    q_groups = queries.reshape(tok_dev, kv_local, group_repeat, HEAD_WIDTH)
    span = tok_dev * max(1, 2048 // tok_dev)

    def attend_block(state, key_piece, value_piece, start):
        count = key_piece.shape[0]
        key_rows = start + jnp.arange(count, dtype=jnp.int32)
        key_pos = storage_positions(key_rows, tok_dev, n_ctx)
        key_doc = document_of(key_pos, doc_ends)
        visible = (query_doc[:, None] == key_doc[None, :]) & (
            key_pos[None, :] <= query_pos[:, None]
        )

        def compute(carry):
            numerator, denominator = carry
            scores = (
                jnp.einsum(
                    "qgrd,kgd->grqk",
                    q_groups,
                    key_piece.reshape(count, kv_local, HEAD_WIDTH),
                    preferred_element_type=jnp.float32,
                )
                * scale
            )
            scores = soft_cap * jnp.tanh(scores / soft_cap)
            weights = jnp.where(visible[None, None], jnp.exp(scores), 0.0)
            numerator = numerator + jnp.einsum(
                "grqk,kgd->grqd",
                weights.astype(jnp.bfloat16),
                value_piece.reshape(count, kv_local, HEAD_WIDTH),
                preferred_element_type=jnp.float32,
            )
            denominator = denominator + jnp.sum(weights, axis=-1)
            return (numerator, denominator)

        return lax.cond(jnp.any(visible), compute, lambda carry: carry, state)

    def attend(state, key_piece, value_piece, start):
        count = key_piece.shape[0]
        if count <= span:
            return attend_block(state, key_piece, value_piece, start)
        blocks = count // span
        whole = blocks * span
        width = key_piece.shape[1]
        key_blocks = key_piece[:whole].reshape(blocks, span, width)
        value_blocks = value_piece[:whole].reshape(blocks, span, width)
        starts = start + span * jnp.arange(blocks, dtype=jnp.int32)

        def step_fn(carry, item):
            return (attend_block(carry, item[0], item[1], item[2]), None)

        state, _ = lax.scan(step_fn, state, (key_blocks, value_blocks, starts))
        if whole < count:
            state = attend_block(state, key_piece[whole:], value_piece[whole:], start + whole)
        return state

    initial = (
        jnp.zeros((kv_local, group_repeat, tok_dev, HEAD_WIDTH), jnp.float32),
        jnp.zeros((kv_local, group_repeat, tok_dev), jnp.float32),
    )
    outer = lax.axis_size("c0")
    inner = lax.axis_size(INNER)
    rows_each = out_weight.shape[0]
    kv_width = keys.shape[1]
    both = gather_tokens(jnp.concatenate([keys, values], axis=1))
    both, out_weight = lax.optimization_barrier((both, out_weight))
    weight_rows = line_gather(out_weight, "c0")
    numerator, denominator = attend(initial, both[:, :kv_width], both[:, kv_width:], jnp.int32(0))
    attended = (numerator / denominator[..., None]).astype(jnp.bfloat16)
    attended = attended.transpose(2, 0, 1, 3).reshape(tok_dev, kv_local * group_repeat * HEAD_WIDTH)
    all_heads = lax.all_gather(attended, "head", axis=1, tiled=True)
    weight_rows = weight_rows.reshape(outer * rows_each, out_weight.shape[1])
    blocks = all_heads.reshape(tok_dev, outer, inner, rows_each).transpose(2, 0, 1, 3)
    regrouped = lax.all_to_all(blocks, INNER, 0, 0, tiled=True)
    partial = jnp.dot(
        regrouped.reshape(inner * tok_dev, outer * rows_each), weight_rows, preferred_element_type=jnp.float32
    )
    mixed = lax.psum_scatter(partial, INNER, scatter_dimension=0, tiled=True)
    squares = lax.psum(jnp.sum(mixed * mixed, axis=1), "head")
    normed = mixed / jnp.sqrt(squares / D + 1e-06)[:, None]
    out32 = hidden_in.astype(jnp.float32) + normed * out_gain[None, :]
    tok_reward = jnp.sum(out32 * reward_weight[None, :], axis=1)
    onehot = (query_doc[:, None] == jnp.arange(NDOC, dtype=jnp.int32)[None, :]).astype(jnp.float32)
    partial_sums = jnp.sum(onehot * tok_reward[:, None], axis=0)
    totals = butterfly_sum(partial_sums, CTX + ("head",))
    rewards = totals / jnp.sqrt(doc_lengths.astype(jnp.float32))
    return (out32.astype(jnp.bfloat16), rewards)


def solution(mesh):
    n_ctx, n_head = mesh.devices.shape
    split = Mesh(mesh.devices.reshape(n_ctx // 4, 2, 2, n_head), CTX + ("head",))
    rows = P(CTX, "head")
    in_specs = (rows, rows, rows, rows, rows, P("head"), P("head"), P())
    out_specs = (rows, P())
    return jax.shard_map(shards, mesh=split, in_specs=in_specs, out_specs=out_specs, check_vma=False)
```

```python
import jax
import jax.numpy as jnp
from jax import lax
from jax.sharding import Mesh, PartitionSpec as P

D = 4608
QUERY_HEADS = 32
KEY_VALUE_HEADS = 16
HEAD_WIDTH = 128
NDOC = 16


soft_cap = 50.0
CTX = ("c0", "c1", "c2")
INNER = ("c1", "c2")


def storage_positions(rows, tok_dev, n_ctx):
    owner = rows // tok_dev
    offset = rows % tok_dev
    half = tok_dev // 2
    slab = jnp.where(offset < half, owner, 2 * n_ctx - 1 - owner)
    return slab * half + offset % half


def document_of(positions, doc_ends):
    return jnp.sum((positions[:, None] >= doc_ends[None, :]).astype(jnp.int32), axis=1)


def ring_gather(x, axis):
    n = lax.axis_size(axis)
    pieces = [x]
    for _ in range(n - 1):
        pieces.append(lax.ppermute(pieces[-1], axis, [(k, (k + 1) % n) for k in range(n)]))
    return jnp.stack(pieces)


def gather_order(x, order):
    stride = {"c2": 1, "c1": lax.axis_size("c2"), "c0": lax.axis_size("c1") * lax.axis_size("c2")}
    source = jnp.zeros((), jnp.int32)
    for axis in order:
        x = ring_gather(x, axis)
        n = lax.axis_size(axis)
        came = (lax.axis_index(axis) - jnp.arange(n, dtype=jnp.int32)) % n
        source = came.reshape((n,) + (1,) * source.ndim) * stride[axis] + source[None]
    return x, source.reshape(-1)


def butterfly_sum(x, axes):
    for axis in axes:
        size = lax.axis_size(axis)
        bit = 1
        while bit < size:
            x = x + lax.ppermute(x, axis, [(i, i ^ bit) for i in range(size)])
            bit *= 2
    return x


def shards(queries, keys, values, hidden_in, out_weight, out_gain, reward_weight, doc_lengths):
    n_ctx = lax.axis_size(CTX)
    device = lax.axis_index(CTX)
    tok_dev = queries.shape[0]
    kv_local = keys.shape[1] // HEAD_WIDTH
    group_repeat = QUERY_HEADS // KEY_VALUE_HEADS
    scale = (D / QUERY_HEADS) ** (-0.5)
    doc_ends = jnp.cumsum(doc_lengths)
    local_rows = device * tok_dev + jnp.arange(tok_dev, dtype=jnp.int32)
    query_pos = storage_positions(local_rows, tok_dev, n_ctx)
    query_doc = document_of(query_pos, doc_ends)
    q_groups = queries.reshape(tok_dev, kv_local, group_repeat, HEAD_WIDTH)
    span = tok_dev * max(1, 2048 // tok_dev)

    def attend_block(state, q_part, key_piece, value_piece, key_rows):
        count = key_piece.shape[0]
        heads = q_part.shape[1]
        key_pos = storage_positions(key_rows, tok_dev, n_ctx)
        key_doc = document_of(key_pos, doc_ends)
        visible = (query_doc[:, None] == key_doc[None, :]) & (
            key_pos[None, :] <= query_pos[:, None]
        )

        def compute(carry):
            numerator, denominator = carry
            scores = (
                jnp.einsum(
                    "qgrd,kgd->grqk",
                    q_part,
                    key_piece.reshape(count, heads, HEAD_WIDTH),
                    preferred_element_type=jnp.float32,
                )
                * scale
            )
            scores = soft_cap * jnp.tanh(scores / soft_cap)
            weights = jnp.where(visible[None, None], jnp.exp(scores), 0.0)
            numerator = numerator + jnp.einsum(
                "grqk,kgd->grqd",
                weights.astype(jnp.bfloat16),
                value_piece.reshape(count, heads, HEAD_WIDTH),
                preferred_element_type=jnp.float32,
            )
            denominator = denominator + jnp.sum(weights, axis=-1)
            return (numerator, denominator)

        return lax.cond(jnp.any(visible), compute, lambda carry: carry, state)

    def attend(q_part, key_piece, value_piece, key_rows):
        heads = q_part.shape[1]
        state = (
            jnp.zeros((heads, group_repeat, tok_dev, HEAD_WIDTH), jnp.float32),
            jnp.zeros((heads, group_repeat, tok_dev), jnp.float32),
        )
        count = key_piece.shape[0]
        if count <= span:
            return attend_block(state, q_part, key_piece, value_piece, key_rows)
        blocks = count // span
        whole = blocks * span
        width = key_piece.shape[1]
        key_blocks = key_piece[:whole].reshape(blocks, span, width)
        value_blocks = value_piece[:whole].reshape(blocks, span, width)
        row_blocks = key_rows[:whole].reshape(blocks, span)

        def step_fn(carry, item):
            return (attend_block(carry, q_part, item[0], item[1], item[2]), None)

        state, _ = lax.scan(step_fn, state, (key_blocks, value_blocks, row_blocks))
        if whole < count:
            state = attend_block(state, q_part, key_piece[whole:], value_piece[whole:], key_rows[whole:])
        return state

    outer = lax.axis_size("c0")
    inner = lax.axis_size(INNER)
    rows_each = out_weight.shape[0]
    weight_rows = lax.all_gather(out_weight, "c0", axis=0, tiled=True)
    half = kv_local // 2
    splits = [(0, half, ("c0", "c2", "c1")), (half, kv_local, ("c0", "c1", "c2"))]
    gathered, bounds = [], []
    for first, last, order in splits:
        if last == first:
            continue
        cols = slice(first * HEAD_WIDTH, last * HEAD_WIDTH)
        got, source = gather_order(jnp.concatenate([keys[:, cols], values[:, cols]], axis=1), order)
        key_rows = (source[:, None] * tok_dev + jnp.arange(tok_dev, dtype=jnp.int32)[None, :]).reshape(-1)
        gathered.append((got.reshape(n_ctx * tok_dev, -1), key_rows))
        bounds.append((first, last))
    gathered, weight_rows = lax.optimization_barrier((gathered, weight_rows))
    numerators, denominators = [], []
    for (first, last), (got, key_rows) in zip(bounds, gathered):
        width = (last - first) * HEAD_WIDTH
        numerator, denominator = attend(q_groups[:, first:last], got[:, :width], got[:, width:], key_rows)
        numerators.append(numerator)
        denominators.append(denominator)
    numerator = jnp.concatenate(numerators, axis=0)
    denominator = jnp.concatenate(denominators, axis=0)
    attended = (numerator / denominator[..., None]).astype(jnp.bfloat16)
    attended = attended.transpose(2, 0, 1, 3).reshape(tok_dev, kv_local * group_repeat * HEAD_WIDTH)
    all_heads = lax.all_gather(attended, "head", axis=1, tiled=True)
    weight_rows = weight_rows.reshape(outer * rows_each, out_weight.shape[1])
    blocks = all_heads.reshape(tok_dev, outer, inner, rows_each).transpose(2, 0, 1, 3)
    regrouped = lax.all_to_all(blocks, INNER, 0, 0, tiled=True)
    partial = jnp.dot(
        regrouped.reshape(inner * tok_dev, outer * rows_each), weight_rows, preferred_element_type=jnp.float32
    )
    mixed = lax.psum_scatter(partial, INNER, scatter_dimension=0, tiled=True)
    squares = lax.psum(jnp.sum(mixed * mixed, axis=1), "head")
    normed = mixed / jnp.sqrt(squares / D + 1e-06)[:, None]
    out32 = hidden_in.astype(jnp.float32) + normed * out_gain[None, :]
    tok_reward = jnp.sum(out32 * reward_weight[None, :], axis=1)
    onehot = (query_doc[:, None] == jnp.arange(NDOC, dtype=jnp.int32)[None, :]).astype(jnp.float32)
    partial_sums = jnp.sum(onehot * tok_reward[:, None], axis=0)
    totals = butterfly_sum(partial_sums, CTX + ("head",))
    rewards = totals / jnp.sqrt(doc_lengths.astype(jnp.float32))
    return (out32.astype(jnp.bfloat16), rewards)


def solution(mesh):
    n_ctx, n_head = mesh.devices.shape
    split = Mesh(mesh.devices.reshape(n_ctx // 4, 2, 2, n_head), CTX + ("head",))
    rows = P(CTX, "head")
    in_specs = (rows, rows, rows, rows, rows, P("head"), P("head"), P())
    out_specs = (rows, P())
    return jax.shard_map(shards, mesh=split, in_specs=in_specs, out_specs=out_specs, check_vma=False)
```

```python
import jax
import jax.numpy as jnp
from jax import lax
from jax.sharding import Mesh, PartitionSpec as P

D = 4608
QUERY_HEADS = 32
KEY_VALUE_HEADS = 16
HEAD_WIDTH = 128
NDOC = 16


soft_cap = 50.0
CTX = ("c0", "c1", "c2")
INNER = ("c1", "c2")


def storage_positions(rows, tok_dev, n_ctx):
    owner = rows // tok_dev
    offset = rows % tok_dev
    half = tok_dev // 2
    slab = jnp.where(offset < half, owner, 2 * n_ctx - 1 - owner)
    return slab * half + offset % half


def document_of(positions, doc_ends):
    return jnp.sum((positions[:, None] >= doc_ends[None, :]).astype(jnp.int32), axis=1)


def ring_gather(x, axis):
    n = lax.axis_size(axis)
    pieces = [x]
    for _ in range(n - 1):
        pieces.append(lax.ppermute(pieces[-1], axis, [(k, (k + 1) % n) for k in range(n)]))
    return jnp.stack(pieces)


def gather_order(x, order):
    stride = {"c2": 1, "c1": lax.axis_size("c2"), "c0": lax.axis_size("c1") * lax.axis_size("c2")}
    source = jnp.zeros((), jnp.int32)
    for axis in order:
        x = ring_gather(x, axis)
        n = lax.axis_size(axis)
        came = (lax.axis_index(axis) - jnp.arange(n, dtype=jnp.int32)) % n
        source = came.reshape((n,) + (1,) * source.ndim) * stride[axis] + source[None]
    return x, source.reshape(-1)


def ring_all_gather(x, axis):
    n = lax.axis_size(axis)
    arrived = ring_gather(x, axis)[::-1]
    return jnp.roll(arrived, lax.axis_index(axis) + 1, axis=0)


def permute_all_to_all(x, axes):
    n = lax.axis_size(axes)
    own = lax.axis_index(axes)
    pieces = [lax.dynamic_index_in_dim(x, own, axis=0, keepdims=False)]
    for shift in range(1, n):
        sent = lax.dynamic_index_in_dim(x, (own + shift) % n, axis=0, keepdims=False)
        pieces.append(lax.ppermute(sent, axes, [(k, (k + shift) % n) for k in range(n)]))
    return jnp.roll(jnp.stack(pieces[::-1]), own + 1, axis=0)


def butterfly_sum(x, axes):
    for axis in axes:
        size = lax.axis_size(axis)
        bit = 1
        while bit < size:
            x = x + lax.ppermute(x, axis, [(i, i ^ bit) for i in range(size)])
            bit *= 2
    return x


def shards(queries, keys, values, hidden_in, out_weight, out_gain, reward_weight, doc_lengths):
    n_ctx = lax.axis_size(CTX)
    device = lax.axis_index(CTX)
    tok_dev = queries.shape[0]
    kv_local = keys.shape[1] // HEAD_WIDTH
    group_repeat = QUERY_HEADS // KEY_VALUE_HEADS
    scale = (D / QUERY_HEADS) ** (-0.5)
    doc_ends = jnp.cumsum(doc_lengths)
    local_rows = device * tok_dev + jnp.arange(tok_dev, dtype=jnp.int32)
    query_pos = storage_positions(local_rows, tok_dev, n_ctx)
    query_doc = document_of(query_pos, doc_ends)
    q_groups = queries.reshape(tok_dev, kv_local, group_repeat, HEAD_WIDTH)
    span = tok_dev * max(1, 2048 // tok_dev)

    def attend_block(state, q_part, key_piece, value_piece, key_rows):
        count = key_piece.shape[0]
        heads = q_part.shape[1]
        key_pos = storage_positions(key_rows, tok_dev, n_ctx)
        key_doc = document_of(key_pos, doc_ends)
        visible = (query_doc[:, None] == key_doc[None, :]) & (
            key_pos[None, :] <= query_pos[:, None]
        )

        def compute(carry):
            numerator, denominator = carry
            scores = (
                jnp.einsum(
                    "qgrd,kgd->grqk",
                    q_part,
                    key_piece.reshape(count, heads, HEAD_WIDTH),
                    preferred_element_type=jnp.float32,
                )
                * scale
            )
            scores = soft_cap * jnp.tanh(scores / soft_cap)
            weights = jnp.where(visible[None, None], jnp.exp(scores), 0.0)
            numerator = numerator + jnp.einsum(
                "grqk,kgd->grqd",
                weights.astype(jnp.bfloat16),
                value_piece.reshape(count, heads, HEAD_WIDTH),
                preferred_element_type=jnp.float32,
            )
            denominator = denominator + jnp.sum(weights, axis=-1)
            return (numerator, denominator)

        return lax.cond(jnp.any(visible), compute, lambda carry: carry, state)

    def attend(q_part, key_piece, value_piece, key_rows):
        heads = q_part.shape[1]
        state = (
            jnp.zeros((heads, group_repeat, tok_dev, HEAD_WIDTH), jnp.float32),
            jnp.zeros((heads, group_repeat, tok_dev), jnp.float32),
        )
        count = key_piece.shape[0]
        if count <= span:
            return attend_block(state, q_part, key_piece, value_piece, key_rows)
        blocks = count // span
        whole = blocks * span
        width = key_piece.shape[1]
        key_blocks = key_piece[:whole].reshape(blocks, span, width)
        value_blocks = value_piece[:whole].reshape(blocks, span, width)
        row_blocks = key_rows[:whole].reshape(blocks, span)

        def step_fn(carry, item):
            return (attend_block(carry, q_part, item[0], item[1], item[2]), None)

        state, _ = lax.scan(step_fn, state, (key_blocks, value_blocks, row_blocks))
        if whole < count:
            state = attend_block(state, q_part, key_piece[whole:], value_piece[whole:], key_rows[whole:])
        return state

    outer = lax.axis_size("c0")
    inner = lax.axis_size(INNER)
    rows_each = out_weight.shape[0]
    weight_rows = lax.all_gather(out_weight, "c0", axis=0, tiled=True)
    half = kv_local // 2
    splits = [(0, half, ("c0", "c2", "c1")), (half, kv_local, ("c0", "c1", "c2"))]
    gathered, bounds = [], []
    for first, last, order in splits:
        if last == first:
            continue
        cols = slice(first * HEAD_WIDTH, last * HEAD_WIDTH)
        got, source = gather_order(jnp.concatenate([keys[:, cols], values[:, cols]], axis=1), order)
        key_rows = (source[:, None] * tok_dev + jnp.arange(tok_dev, dtype=jnp.int32)[None, :]).reshape(-1)
        gathered.append((got.reshape(n_ctx * tok_dev, -1), key_rows))
        bounds.append((first, last))
    gathered, weight_rows = lax.optimization_barrier((gathered, weight_rows))
    numerators, denominators = [], []
    for (first, last), (got, key_rows) in zip(bounds, gathered):
        width = (last - first) * HEAD_WIDTH
        numerator, denominator = attend(q_groups[:, first:last], got[:, :width], got[:, width:], key_rows)
        numerators.append(numerator)
        denominators.append(denominator)
    numerator = jnp.concatenate(numerators, axis=0)
    denominator = jnp.concatenate(denominators, axis=0)
    attended = (numerator / denominator[..., None]).astype(jnp.bfloat16)
    attended = attended.transpose(2, 0, 1, 3).reshape(tok_dev, kv_local * group_repeat * HEAD_WIDTH)
    all_heads = ring_all_gather(attended, "head").transpose(1, 0, 2).reshape(tok_dev, -1)
    weight_rows = weight_rows.reshape(outer * rows_each, out_weight.shape[1])
    blocks = all_heads.reshape(tok_dev, outer, inner, rows_each).transpose(2, 0, 1, 3)
    regrouped = permute_all_to_all(blocks, INNER)
    partial = jnp.dot(
        regrouped.reshape(inner * tok_dev, outer * rows_each), weight_rows, preferred_element_type=jnp.float32
    )
    mixed = lax.psum_scatter(partial, INNER, scatter_dimension=0, tiled=True)
    squares = lax.psum(jnp.sum(mixed * mixed, axis=1), "head")
    normed = mixed / jnp.sqrt(squares / D + 1e-06)[:, None]
    out32 = hidden_in.astype(jnp.float32) + normed * out_gain[None, :]
    tok_reward = jnp.sum(out32 * reward_weight[None, :], axis=1)
    onehot = (query_doc[:, None] == jnp.arange(NDOC, dtype=jnp.int32)[None, :]).astype(jnp.float32)
    partial_sums = jnp.sum(onehot * tok_reward[:, None], axis=0)
    totals = butterfly_sum(partial_sums, CTX + ("head",))
    rewards = totals / jnp.sqrt(doc_lengths.astype(jnp.float32))
    return (out32.astype(jnp.bfloat16), rewards)


def solution(mesh):
    n_ctx, n_head = mesh.devices.shape
    split = Mesh(mesh.devices.reshape(n_ctx // 4, 2, 2, n_head), CTX + ("head",))
    rows = P(CTX, "head")
    in_specs = (rows, rows, rows, rows, rows, P("head"), P("head"), P())
    out_specs = (rows, P())
    return jax.shard_map(shards, mesh=split, in_specs=in_specs, out_specs=out_specs, check_vma=False)
```

```python
import jax
import jax.numpy as jnp
from jax import lax
from jax.sharding import Mesh, PartitionSpec as P

D = 4608
QUERY_HEADS = 32
KEY_VALUE_HEADS = 16
HEAD_WIDTH = 128
NDOC = 16


soft_cap = 50.0
CTX = ("c0", "c1", "c2")
INNER = ("c1", "c2")


def storage_positions(rows, tok_dev, n_ctx):
    owner = rows // tok_dev
    offset = rows % tok_dev
    half = tok_dev // 2
    slab = jnp.where(offset < half, owner, 2 * n_ctx - 1 - owner)
    return slab * half + offset % half


def document_of(positions, doc_ends):
    return jnp.sum((positions[:, None] >= doc_ends[None, :]).astype(jnp.int32), axis=1)


def ring_gather(x, axis):
    n = lax.axis_size(axis)
    pieces = [x]
    for _ in range(n - 1):
        pieces.append(lax.ppermute(pieces[-1], axis, [(k, (k + 1) % n) for k in range(n)]))
    return jnp.stack(pieces)


def gather_order(x, order):
    stride = {"c2": 1, "c1": lax.axis_size("c2"), "c0": lax.axis_size("c1") * lax.axis_size("c2")}
    source = jnp.zeros((), jnp.int32)
    for axis in order:
        x = ring_gather(x, axis)
        n = lax.axis_size(axis)
        came = (lax.axis_index(axis) - jnp.arange(n, dtype=jnp.int32)) % n
        source = came.reshape((n,) + (1,) * source.ndim) * stride[axis] + source[None]
    return x, source.reshape(-1)


def ring_all_gather(x, axis):
    n = lax.axis_size(axis)
    arrived = ring_gather(x, axis)[::-1]
    return jnp.roll(arrived, lax.axis_index(axis) + 1, axis=0)


def permute_all_to_all(x, axes):
    n = lax.axis_size(axes)
    own = lax.axis_index(axes)
    pieces = [lax.dynamic_index_in_dim(x, own, axis=0, keepdims=False)]
    for shift in range(1, n):
        sent = lax.dynamic_index_in_dim(x, (own + shift) % n, axis=0, keepdims=False)
        pieces.append(lax.ppermute(sent, axes, [(k, (k + shift) % n) for k in range(n)]))
    return jnp.roll(jnp.stack(pieces[::-1]), own + 1, axis=0)


def butterfly_sum(x, axes):
    for axis in axes:
        size = lax.axis_size(axis)
        bit = 1
        while bit < size:
            x = x + lax.ppermute(x, axis, [(i, i ^ bit) for i in range(size)])
            bit *= 2
    return x


def shards(queries, keys, values, hidden_in, out_weight, out_gain, reward_weight, doc_lengths):
    n_ctx = lax.axis_size(CTX)
    device = lax.axis_index(CTX)
    tok_dev = queries.shape[0]
    kv_local = keys.shape[1] // HEAD_WIDTH
    group_repeat = QUERY_HEADS // KEY_VALUE_HEADS
    scale = (D / QUERY_HEADS) ** (-0.5)
    doc_ends = jnp.cumsum(doc_lengths)
    local_rows = device * tok_dev + jnp.arange(tok_dev, dtype=jnp.int32)
    query_pos = storage_positions(local_rows, tok_dev, n_ctx)
    query_doc = document_of(query_pos, doc_ends)
    q_groups = queries.reshape(tok_dev, kv_local, group_repeat, HEAD_WIDTH)
    span = tok_dev * max(1, 2048 // tok_dev)

    def attend_block(state, q_part, key_piece, value_piece, key_rows):
        count = key_piece.shape[0]
        heads = q_part.shape[1]
        key_pos = storage_positions(key_rows, tok_dev, n_ctx)
        key_doc = document_of(key_pos, doc_ends)
        visible = (query_doc[:, None] == key_doc[None, :]) & (
            key_pos[None, :] <= query_pos[:, None]
        )

        def compute(carry):
            numerator, denominator = carry
            scores = (
                jnp.einsum(
                    "qgrd,kgd->grqk",
                    q_part,
                    key_piece.reshape(count, heads, HEAD_WIDTH),
                    preferred_element_type=jnp.float32,
                )
                * scale
            )
            scores = soft_cap * jnp.tanh(scores / soft_cap)
            weights = jnp.where(visible[None, None], jnp.exp(scores), 0.0)
            numerator = numerator + jnp.einsum(
                "grqk,kgd->grqd",
                weights.astype(jnp.bfloat16),
                value_piece.reshape(count, heads, HEAD_WIDTH),
                preferred_element_type=jnp.float32,
            )
            denominator = denominator + jnp.sum(weights, axis=-1)
            return (numerator, denominator)

        return lax.cond(jnp.any(visible), compute, lambda carry: carry, state)

    def attend(q_part, key_piece, value_piece, key_rows):
        heads = q_part.shape[1]
        state = (
            jnp.zeros((heads, group_repeat, tok_dev, HEAD_WIDTH), jnp.float32),
            jnp.zeros((heads, group_repeat, tok_dev), jnp.float32),
        )
        count = key_piece.shape[0]
        if count <= span:
            return attend_block(state, q_part, key_piece, value_piece, key_rows)
        blocks = count // span
        whole = blocks * span
        width = key_piece.shape[1]
        key_blocks = key_piece[:whole].reshape(blocks, span, width)
        value_blocks = value_piece[:whole].reshape(blocks, span, width)
        row_blocks = key_rows[:whole].reshape(blocks, span)

        def step_fn(carry, item):
            return (attend_block(carry, q_part, item[0], item[1], item[2]), None)

        state, _ = lax.scan(step_fn, state, (key_blocks, value_blocks, row_blocks))
        if whole < count:
            state = attend_block(state, q_part, key_piece[whole:], value_piece[whole:], key_rows[whole:])
        return state

    outer = lax.axis_size("c0")
    inner = lax.axis_size(INNER)
    rows_each = out_weight.shape[0]
    weight_rows = lax.all_gather(out_weight, "c0", axis=0, tiled=True)
    half = kv_local // 2
    splits = [(0, half, ("c0", "c2", "c1")), (half, kv_local, ("c0", "c1", "c2"))]
    gathered, bounds = [], []
    for first, last, order in splits:
        if last == first:
            continue
        cols = slice(first * HEAD_WIDTH, last * HEAD_WIDTH)
        got, source = gather_order(jnp.concatenate([keys[:, cols], values[:, cols]], axis=1), order)
        key_rows = (source[:, None] * tok_dev + jnp.arange(tok_dev, dtype=jnp.int32)[None, :]).reshape(-1)
        gathered.append((got.reshape(n_ctx * tok_dev, -1), key_rows))
        bounds.append((first, last))
    gathered, weight_rows = lax.optimization_barrier((gathered, weight_rows))
    numerators, denominators = [], []
    for (first, last), (got, key_rows) in zip(bounds, gathered):
        width = (last - first) * HEAD_WIDTH
        numerator, denominator = attend(q_groups[:, first:last], got[:, :width], got[:, width:], key_rows)
        numerators.append(numerator)
        denominators.append(denominator)
    numerator = jnp.concatenate(numerators, axis=0)
    denominator = jnp.concatenate(denominators, axis=0)
    attended = (numerator / denominator[..., None]).astype(jnp.bfloat16)
    attended = attended.transpose(2, 0, 1, 3).reshape(tok_dev, kv_local * group_repeat * HEAD_WIDTH)
    all_heads = ring_all_gather(attended, "head").transpose(1, 0, 2).reshape(tok_dev, -1)
    weight_rows = weight_rows.reshape(outer * rows_each, out_weight.shape[1])
    blocks = all_heads.reshape(tok_dev, outer, inner, rows_each).transpose(2, 0, 1, 3)
    regrouped = permute_all_to_all(blocks, INNER)
    partial = jnp.dot(
        regrouped.reshape(inner * tok_dev, outer * rows_each), weight_rows, preferred_element_type=jnp.float32
    )
    mixed = lax.psum_scatter(partial.astype(jnp.bfloat16), INNER, scatter_dimension=0, tiled=True)
    mixed = mixed.astype(jnp.float32)
    squares = lax.psum(jnp.sum(mixed * mixed, axis=1), "head")
    normed = mixed / jnp.sqrt(squares / D + 1e-06)[:, None]
    out32 = hidden_in.astype(jnp.float32) + normed * out_gain[None, :]
    tok_reward = jnp.sum(out32 * reward_weight[None, :], axis=1)
    onehot = (query_doc[:, None] == jnp.arange(NDOC, dtype=jnp.int32)[None, :]).astype(jnp.float32)
    partial_sums = jnp.sum(onehot * tok_reward[:, None], axis=0)
    totals = butterfly_sum(partial_sums, CTX + ("head",))
    rewards = totals / jnp.sqrt(doc_lengths.astype(jnp.float32))
    return (out32.astype(jnp.bfloat16), rewards)


def solution(mesh):
    n_ctx, n_head = mesh.devices.shape
    split = Mesh(mesh.devices.reshape(n_ctx // 4, 2, 2, n_head), CTX + ("head",))
    rows = P(CTX, "head")
    in_specs = (rows, rows, rows, rows, rows, P("head"), P("head"), P())
    out_specs = (rows, P())
    return jax.shard_map(shards, mesh=split, in_specs=in_specs, out_specs=out_specs, check_vma=False)
```

```python
import jax
import jax.numpy as jnp
from jax import lax
from jax.sharding import Mesh, PartitionSpec as P

D = 4608
QUERY_HEADS = 32
KEY_VALUE_HEADS = 16
HEAD_WIDTH = 128
NDOC = 16


soft_cap = 50.0
CTX = ("c0", "c1", "c2")
OUTER = ("c0", "c2")


def storage_positions(rows, tok_dev, n_ctx):
    owner = rows // tok_dev
    offset = rows % tok_dev
    half = tok_dev // 2
    slab = jnp.where(offset < half, owner, 2 * n_ctx - 1 - owner)
    return slab * half + offset % half


def document_of(positions, doc_ends):
    return jnp.sum((positions[:, None] >= doc_ends[None, :]).astype(jnp.int32), axis=1)


def ring_gather(x, axis):
    n = lax.axis_size(axis)
    pieces = [x]
    for _ in range(n - 1):
        pieces.append(lax.ppermute(pieces[-1], axis, [(k, (k + 1) % n) for k in range(n)]))
    return jnp.stack(pieces)


def gather_order(x, order):
    stride = {"c2": 1, "c1": lax.axis_size("c2"), "c0": lax.axis_size("c1") * lax.axis_size("c2")}
    source = jnp.zeros((), jnp.int32)
    for axis in order:
        x = ring_gather(x, axis)
        n = lax.axis_size(axis)
        came = (lax.axis_index(axis) - jnp.arange(n, dtype=jnp.int32)) % n
        source = came.reshape((n,) + (1,) * source.ndim) * stride[axis] + source[None]
    return x, source.reshape(-1)


def ring_all_gather(x, axis):
    n = lax.axis_size(axis)
    arrived = ring_gather(x, axis)[::-1]
    return jnp.roll(arrived, lax.axis_index(axis) + 1, axis=0)


def permute_all_to_all(x, axes):
    n = lax.axis_size(axes)
    own = lax.axis_index(axes)
    pieces = [lax.dynamic_index_in_dim(x, own, axis=0, keepdims=False)]
    for shift in range(1, n):
        sent = lax.dynamic_index_in_dim(x, (own + shift) % n, axis=0, keepdims=False)
        pieces.append(lax.ppermute(sent, axes, [(k, (k + shift) % n) for k in range(n)]))
    return jnp.roll(jnp.stack(pieces[::-1]), own + 1, axis=0)


def butterfly_sum(x, axes):
    for axis in axes:
        size = lax.axis_size(axis)
        bit = 1
        while bit < size:
            x = x + lax.ppermute(x, axis, [(i, i ^ bit) for i in range(size)])
            bit *= 2
    return x


def shards(queries, keys, values, hidden_in, out_weight, out_gain, reward_weight, doc_lengths):
    n_ctx = lax.axis_size(CTX)
    device = lax.axis_index(CTX)
    tok_dev = queries.shape[0]
    kv_local = keys.shape[1] // HEAD_WIDTH
    group_repeat = QUERY_HEADS // KEY_VALUE_HEADS
    scale = (D / QUERY_HEADS) ** (-0.5)
    doc_ends = jnp.cumsum(doc_lengths)
    local_rows = device * tok_dev + jnp.arange(tok_dev, dtype=jnp.int32)
    query_pos = storage_positions(local_rows, tok_dev, n_ctx)
    query_doc = document_of(query_pos, doc_ends)
    q_groups = queries.reshape(tok_dev, kv_local, group_repeat, HEAD_WIDTH)
    span = tok_dev * max(1, 2048 // tok_dev)

    def attend_block(state, q_part, key_piece, value_piece, key_rows):
        count = key_piece.shape[0]
        heads = q_part.shape[1]
        key_pos = storage_positions(key_rows, tok_dev, n_ctx)
        key_doc = document_of(key_pos, doc_ends)
        visible = (query_doc[:, None] == key_doc[None, :]) & (
            key_pos[None, :] <= query_pos[:, None]
        )

        def compute(carry):
            numerator, denominator = carry
            scores = (
                jnp.einsum(
                    "qgrd,kgd->grqk",
                    q_part,
                    key_piece.reshape(count, heads, HEAD_WIDTH),
                    preferred_element_type=jnp.float32,
                )
                * scale
            )
            scores = soft_cap * jnp.tanh(scores / soft_cap)
            weights = jnp.where(visible[None, None], jnp.exp(scores), 0.0)
            numerator = numerator + jnp.einsum(
                "grqk,kgd->grqd",
                weights.astype(jnp.bfloat16),
                value_piece.reshape(count, heads, HEAD_WIDTH),
                preferred_element_type=jnp.float32,
            )
            denominator = denominator + jnp.sum(weights, axis=-1)
            return (numerator, denominator)

        return lax.cond(jnp.any(visible), compute, lambda carry: carry, state)

    def attend(q_part, key_piece, value_piece, key_rows):
        heads = q_part.shape[1]
        state = (
            jnp.zeros((heads, group_repeat, tok_dev, HEAD_WIDTH), jnp.float32),
            jnp.zeros((heads, group_repeat, tok_dev), jnp.float32),
        )
        count = key_piece.shape[0]
        if count <= span:
            return attend_block(state, q_part, key_piece, value_piece, key_rows)
        blocks = count // span
        whole = blocks * span
        width = key_piece.shape[1]
        key_blocks = key_piece[:whole].reshape(blocks, span, width)
        value_blocks = value_piece[:whole].reshape(blocks, span, width)
        row_blocks = key_rows[:whole].reshape(blocks, span)

        def step_fn(carry, item):
            return (attend_block(carry, q_part, item[0], item[1], item[2]), None)

        state, _ = lax.scan(step_fn, state, (key_blocks, value_blocks, row_blocks))
        if whole < count:
            state = attend_block(state, q_part, key_piece[whole:], value_piece[whole:], key_rows[whole:])
        return state

    rows_each = out_weight.shape[0]
    weight_rows = lax.all_gather(out_weight, OUTER, axis=0, tiled=True)
    half = kv_local // 2
    splits = [(0, half, ("c0", "c2", "c1")), (half, kv_local, ("c0", "c1", "c2"))]
    gathered, bounds = [], []
    for first, last, order in splits:
        if last == first:
            continue
        cols = slice(first * HEAD_WIDTH, last * HEAD_WIDTH)
        got, source = gather_order(jnp.concatenate([keys[:, cols], values[:, cols]], axis=1), order)
        key_rows = (source[:, None] * tok_dev + jnp.arange(tok_dev, dtype=jnp.int32)[None, :]).reshape(-1)
        gathered.append((got.reshape(n_ctx * tok_dev, -1), key_rows))
        bounds.append((first, last))
    gathered, weight_rows = lax.optimization_barrier((gathered, weight_rows))
    numerators, denominators = [], []
    for (first, last), (got, key_rows) in zip(bounds, gathered):
        width = (last - first) * HEAD_WIDTH
        numerator, denominator = attend(q_groups[:, first:last], got[:, :width], got[:, width:], key_rows)
        numerators.append(numerator)
        denominators.append(denominator)
    numerator = jnp.concatenate(numerators, axis=0)
    denominator = jnp.concatenate(denominators, axis=0)
    attended = (numerator / denominator[..., None]).astype(jnp.bfloat16)
    attended = attended.transpose(2, 0, 1, 3).reshape(tok_dev, kv_local * group_repeat * HEAD_WIDTH)
    all_heads = ring_all_gather(attended, "head").transpose(1, 0, 2).reshape(tok_dev, -1)
    n0 = lax.axis_size("c0")
    n1 = lax.axis_size("c1")
    n2 = lax.axis_size("c2")
    weight_rows = weight_rows.reshape(n0 * n2 * rows_each, out_weight.shape[1])
    blocks = all_heads.reshape(tok_dev, n0, n1, n2, rows_each).transpose(2, 0, 1, 3, 4)
    regrouped = permute_all_to_all(blocks, "c1")
    partial = jnp.dot(
        regrouped.reshape(n1 * tok_dev, n0 * n2 * rows_each), weight_rows, preferred_element_type=jnp.float32
    )
    mixed = lax.psum_scatter(partial, "c1", scatter_dimension=0, tiled=True)
    squares = lax.psum(jnp.sum(mixed * mixed, axis=1), "head")
    normed = mixed / jnp.sqrt(squares / D + 1e-06)[:, None]
    out32 = hidden_in.astype(jnp.float32) + normed * out_gain[None, :]
    tok_reward = jnp.sum(out32 * reward_weight[None, :], axis=1)
    onehot = (query_doc[:, None] == jnp.arange(NDOC, dtype=jnp.int32)[None, :]).astype(jnp.float32)
    partial_sums = jnp.sum(onehot * tok_reward[:, None], axis=0)
    totals = butterfly_sum(partial_sums, CTX + ("head",))
    rewards = totals / jnp.sqrt(doc_lengths.astype(jnp.float32))
    return (out32.astype(jnp.bfloat16), rewards)


def solution(mesh):
    n_ctx, n_head = mesh.devices.shape
    split = Mesh(mesh.devices.reshape(n_ctx // 4, 2, 2, n_head), CTX + ("head",))
    rows = P(CTX, "head")
    in_specs = (rows, rows, rows, rows, rows, P("head"), P("head"), P())
    out_specs = (rows, P())
    return jax.shard_map(shards, mesh=split, in_specs=in_specs, out_specs=out_specs, check_vma=False)
```

```python
import jax
import jax.numpy as jnp
from jax import lax
from jax.sharding import Mesh, PartitionSpec as P

D = 4608
QUERY_HEADS = 32
KEY_VALUE_HEADS = 16
HEAD_WIDTH = 128
NDOC = 16


soft_cap = 50.0
CTX = ("c0", "c1", "c2")
INNER = ("c1", "c2")


def storage_positions(rows, tok_dev, n_ctx):
    owner = rows // tok_dev
    offset = rows % tok_dev
    half = tok_dev // 2
    slab = jnp.where(offset < half, owner, 2 * n_ctx - 1 - owner)
    return slab * half + offset % half


def document_of(positions, doc_ends):
    return jnp.sum((positions[:, None] >= doc_ends[None, :]).astype(jnp.int32), axis=1)


def ring_gather(x, axis):
    n = lax.axis_size(axis)
    pieces = [x]
    for _ in range(n - 1):
        pieces.append(lax.ppermute(pieces[-1], axis, [(k, (k + 1) % n) for k in range(n)]))
    return jnp.stack(pieces)


def gather_order(x, order):
    stride = {"c2": 1, "c1": lax.axis_size("c2"), "c0": lax.axis_size("c1") * lax.axis_size("c2")}
    source = jnp.zeros((), jnp.int32)
    for axis in order:
        x = ring_gather(x, axis)
        n = lax.axis_size(axis)
        came = (lax.axis_index(axis) - jnp.arange(n, dtype=jnp.int32)) % n
        source = came.reshape((n,) + (1,) * source.ndim) * stride[axis] + source[None]
    return x, source.reshape(-1)


def ring_all_gather(x, axis):
    n = lax.axis_size(axis)
    arrived = ring_gather(x, axis)[::-1]
    return jnp.roll(arrived, lax.axis_index(axis) + 1, axis=0)


def permute_all_to_all(x, axes):
    n = lax.axis_size(axes)
    own = lax.axis_index(axes)
    pieces = [lax.dynamic_index_in_dim(x, own, axis=0, keepdims=False)]
    for shift in range(1, n):
        sent = lax.dynamic_index_in_dim(x, (own + shift) % n, axis=0, keepdims=False)
        pieces.append(lax.ppermute(sent, axes, [(k, (k + shift) % n) for k in range(n)]))
    return jnp.roll(jnp.stack(pieces[::-1]), own + 1, axis=0)


def permute_reduce_scatter(x, axes):
    n = lax.axis_size(axes)
    own = lax.axis_index(axes)
    total = lax.dynamic_index_in_dim(x, own, axis=0, keepdims=False)
    for shift in range(1, n):
        sent = lax.dynamic_index_in_dim(x, (own + shift) % n, axis=0, keepdims=False)
        total = total + lax.ppermute(sent, axes, [(k, (k + shift) % n) for k in range(n)])
    return total


def butterfly_sum(x, axes):
    for axis in axes:
        size = lax.axis_size(axis)
        bit = 1
        while bit < size:
            x = x + lax.ppermute(x, axis, [(i, i ^ bit) for i in range(size)])
            bit *= 2
    return x


def shards(queries, keys, values, hidden_in, out_weight, out_gain, reward_weight, doc_lengths):
    n_ctx = lax.axis_size(CTX)
    device = lax.axis_index(CTX)
    tok_dev = queries.shape[0]
    kv_local = keys.shape[1] // HEAD_WIDTH
    group_repeat = QUERY_HEADS // KEY_VALUE_HEADS
    scale = (D / QUERY_HEADS) ** (-0.5)
    doc_ends = jnp.cumsum(doc_lengths)
    local_rows = device * tok_dev + jnp.arange(tok_dev, dtype=jnp.int32)
    query_pos = storage_positions(local_rows, tok_dev, n_ctx)
    query_doc = document_of(query_pos, doc_ends)
    q_groups = queries.reshape(tok_dev, kv_local, group_repeat, HEAD_WIDTH)
    span = tok_dev * max(1, 2048 // tok_dev)

    def attend_block(state, q_part, key_piece, value_piece, key_rows):
        count = key_piece.shape[0]
        heads = q_part.shape[1]
        key_pos = storage_positions(key_rows, tok_dev, n_ctx)
        key_doc = document_of(key_pos, doc_ends)
        visible = (query_doc[:, None] == key_doc[None, :]) & (
            key_pos[None, :] <= query_pos[:, None]
        )

        def compute(carry):
            numerator, denominator = carry
            scores = (
                jnp.einsum(
                    "qgrd,kgd->grqk",
                    q_part,
                    key_piece.reshape(count, heads, HEAD_WIDTH),
                    preferred_element_type=jnp.float32,
                )
                * scale
            )
            scores = soft_cap * jnp.tanh(scores / soft_cap)
            weights = jnp.where(visible[None, None], jnp.exp(scores), 0.0)
            numerator = numerator + jnp.einsum(
                "grqk,kgd->grqd",
                weights.astype(jnp.bfloat16),
                value_piece.reshape(count, heads, HEAD_WIDTH),
                preferred_element_type=jnp.float32,
            )
            denominator = denominator + jnp.sum(weights, axis=-1)
            return (numerator, denominator)

        return lax.cond(jnp.any(visible), compute, lambda carry: carry, state)

    def attend(q_part, key_piece, value_piece, key_rows):
        heads = q_part.shape[1]
        state = (
            jnp.zeros((heads, group_repeat, tok_dev, HEAD_WIDTH), jnp.float32),
            jnp.zeros((heads, group_repeat, tok_dev), jnp.float32),
        )
        count = key_piece.shape[0]
        if count <= span:
            return attend_block(state, q_part, key_piece, value_piece, key_rows)
        blocks = count // span
        whole = blocks * span
        width = key_piece.shape[1]
        key_blocks = key_piece[:whole].reshape(blocks, span, width)
        value_blocks = value_piece[:whole].reshape(blocks, span, width)
        row_blocks = key_rows[:whole].reshape(blocks, span)

        def step_fn(carry, item):
            return (attend_block(carry, q_part, item[0], item[1], item[2]), None)

        state, _ = lax.scan(step_fn, state, (key_blocks, value_blocks, row_blocks))
        if whole < count:
            state = attend_block(state, q_part, key_piece[whole:], value_piece[whole:], key_rows[whole:])
        return state

    outer = lax.axis_size("c0")
    inner = lax.axis_size(INNER)
    rows_each = out_weight.shape[0]
    weight_rows = lax.all_gather(out_weight, "c0", axis=0, tiled=True)
    half = kv_local // 2
    splits = [(0, half, ("c0", "c2", "c1")), (half, kv_local, ("c0", "c1", "c2"))]
    gathered, bounds = [], []
    for first, last, order in splits:
        if last == first:
            continue
        cols = slice(first * HEAD_WIDTH, last * HEAD_WIDTH)
        got, source = gather_order(jnp.concatenate([keys[:, cols], values[:, cols]], axis=1), order)
        key_rows = (source[:, None] * tok_dev + jnp.arange(tok_dev, dtype=jnp.int32)[None, :]).reshape(-1)
        gathered.append((got.reshape(n_ctx * tok_dev, -1), key_rows))
        bounds.append((first, last))
    gathered, weight_rows = lax.optimization_barrier((gathered, weight_rows))
    numerators, denominators = [], []
    for (first, last), (got, key_rows) in zip(bounds, gathered):
        width = (last - first) * HEAD_WIDTH
        numerator, denominator = attend(q_groups[:, first:last], got[:, :width], got[:, width:], key_rows)
        numerators.append(numerator)
        denominators.append(denominator)
    numerator = jnp.concatenate(numerators, axis=0)
    denominator = jnp.concatenate(denominators, axis=0)
    attended = (numerator / denominator[..., None]).astype(jnp.bfloat16)
    attended = attended.transpose(2, 0, 1, 3).reshape(tok_dev, kv_local * group_repeat * HEAD_WIDTH)
    all_heads = ring_all_gather(attended, "head").transpose(1, 0, 2).reshape(tok_dev, -1)
    weight_rows = weight_rows.reshape(outer * rows_each, out_weight.shape[1])
    blocks = all_heads.reshape(tok_dev, outer, inner, rows_each).transpose(2, 0, 1, 3)
    regrouped = permute_all_to_all(blocks, INNER)
    partial = jnp.dot(
        regrouped.reshape(inner * tok_dev, outer * rows_each), weight_rows, preferred_element_type=jnp.float32
    )
    mixed = permute_reduce_scatter(partial.reshape(inner, tok_dev, -1), INNER)
    squares = lax.psum(jnp.sum(mixed * mixed, axis=1), "head")
    normed = mixed / jnp.sqrt(squares / D + 1e-06)[:, None]
    out32 = hidden_in.astype(jnp.float32) + normed * out_gain[None, :]
    tok_reward = jnp.sum(out32 * reward_weight[None, :], axis=1)
    onehot = (query_doc[:, None] == jnp.arange(NDOC, dtype=jnp.int32)[None, :]).astype(jnp.float32)
    partial_sums = jnp.sum(onehot * tok_reward[:, None], axis=0)
    totals = butterfly_sum(partial_sums, CTX + ("head",))
    rewards = totals / jnp.sqrt(doc_lengths.astype(jnp.float32))
    return (out32.astype(jnp.bfloat16), rewards)


def solution(mesh):
    n_ctx, n_head = mesh.devices.shape
    split = Mesh(mesh.devices.reshape(n_ctx // 4, 2, 2, n_head), CTX + ("head",))
    rows = P(CTX, "head")
    in_specs = (rows, rows, rows, rows, rows, P("head"), P("head"), P())
    out_specs = (rows, P())
    return jax.shard_map(shards, mesh=split, in_specs=in_specs, out_specs=out_specs, check_vma=False)
```

```python
import jax
import jax.numpy as jnp
from jax import lax
from jax.sharding import Mesh, PartitionSpec as P

D = 4608
QUERY_HEADS = 32
KEY_VALUE_HEADS = 16
HEAD_WIDTH = 128
NDOC = 16


soft_cap = 50.0
CTX = ("c0", "c1", "c2")
INNER = ("c1", "c2")


def storage_positions(rows, tok_dev, n_ctx):
    owner = rows // tok_dev
    offset = rows % tok_dev
    half = tok_dev // 2
    slab = jnp.where(offset < half, owner, 2 * n_ctx - 1 - owner)
    return slab * half + offset % half


def document_of(positions, doc_ends):
    return jnp.sum((positions[:, None] >= doc_ends[None, :]).astype(jnp.int32), axis=1)


def ring_gather(x, axis):
    n = lax.axis_size(axis)
    pieces = [x]
    for _ in range(n - 1):
        pieces.append(lax.ppermute(pieces[-1], axis, [(k, (k + 1) % n) for k in range(n)]))
    return jnp.stack(pieces)


def gather_order(x, order):
    stride = {"c2": 1, "c1": lax.axis_size("c2"), "c0": lax.axis_size("c1") * lax.axis_size("c2")}
    source = jnp.zeros((), jnp.int32)
    for axis in order:
        x = ring_gather(x, axis)
        n = lax.axis_size(axis)
        came = (lax.axis_index(axis) - jnp.arange(n, dtype=jnp.int32)) % n
        source = came.reshape((n,) + (1,) * source.ndim) * stride[axis] + source[None]
    return x, source.reshape(-1)


def ring_all_gather(x, axis):
    n = lax.axis_size(axis)
    arrived = ring_gather(x, axis)[::-1]
    return jnp.roll(arrived, lax.axis_index(axis) + 1, axis=0)


def permute_all_to_all(x, axes):
    n = lax.axis_size(axes)
    own = lax.axis_index(axes)
    pieces = [lax.dynamic_index_in_dim(x, own, axis=0, keepdims=False)]
    for shift in range(1, n):
        sent = lax.dynamic_index_in_dim(x, (own + shift) % n, axis=0, keepdims=False)
        pieces.append(lax.ppermute(sent, axes, [(k, (k + shift) % n) for k in range(n)]))
    return jnp.roll(jnp.stack(pieces[::-1]), own + 1, axis=0)


def permute_reduce_scatter(x, axes):
    n = lax.axis_size(axes)
    own = lax.axis_index(axes)
    total = lax.dynamic_index_in_dim(x, own, axis=0, keepdims=False)
    for shift in range(1, n):
        sent = lax.dynamic_index_in_dim(x, (own + shift) % n, axis=0, keepdims=False)
        total = total + lax.ppermute(sent, axes, [(k, (k + shift) % n) for k in range(n)])
    return total


def butterfly_sum(x, axes):
    for axis in axes:
        size = lax.axis_size(axis)
        bit = 1
        while bit < size:
            x = x + lax.ppermute(x, axis, [(i, i ^ bit) for i in range(size)])
            bit *= 2
    return x


def shards(queries, keys, values, hidden_in, out_weight, out_gain, reward_weight, doc_lengths):
    n_ctx = lax.axis_size(CTX)
    device = lax.axis_index(CTX)
    tok_dev = queries.shape[0]
    kv_local = keys.shape[1] // HEAD_WIDTH
    group_repeat = QUERY_HEADS // KEY_VALUE_HEADS
    scale = (D / QUERY_HEADS) ** (-0.5)
    doc_ends = jnp.cumsum(doc_lengths)
    local_rows = device * tok_dev + jnp.arange(tok_dev, dtype=jnp.int32)
    query_pos = storage_positions(local_rows, tok_dev, n_ctx)
    query_doc = document_of(query_pos, doc_ends)
    q_groups = queries.reshape(tok_dev, kv_local, group_repeat, HEAD_WIDTH)
    span = tok_dev * max(1, 2048 // tok_dev)

    def attend_block(state, q_part, key_piece, value_piece, key_rows):
        count = key_piece.shape[0]
        heads = q_part.shape[1]
        key_pos = storage_positions(key_rows, tok_dev, n_ctx)
        key_doc = document_of(key_pos, doc_ends)
        visible = (query_doc[:, None] == key_doc[None, :]) & (
            key_pos[None, :] <= query_pos[:, None]
        )

        def compute(carry):
            numerator, denominator = carry
            scores = (
                jnp.einsum(
                    "qgrd,kgd->grqk",
                    q_part,
                    key_piece.reshape(count, heads, HEAD_WIDTH),
                    preferred_element_type=jnp.float32,
                )
                * scale
            )
            scores = soft_cap * jnp.tanh(scores / soft_cap)
            weights = jnp.where(visible[None, None], jnp.exp(scores), 0.0)
            numerator = numerator + jnp.einsum(
                "grqk,kgd->grqd",
                weights.astype(jnp.bfloat16),
                value_piece.reshape(count, heads, HEAD_WIDTH),
                preferred_element_type=jnp.float32,
            )
            denominator = denominator + jnp.sum(weights, axis=-1)
            return (numerator, denominator)

        return lax.cond(jnp.any(visible), compute, lambda carry: carry, state)

    def attend(q_part, key_piece, value_piece, key_rows):
        heads = q_part.shape[1]
        state = (
            jnp.zeros((heads, group_repeat, tok_dev, HEAD_WIDTH), jnp.float32),
            jnp.zeros((heads, group_repeat, tok_dev), jnp.float32),
        )
        count = key_piece.shape[0]
        if count <= span:
            return attend_block(state, q_part, key_piece, value_piece, key_rows)
        blocks = count // span
        whole = blocks * span
        width = key_piece.shape[1]
        key_blocks = key_piece[:whole].reshape(blocks, span, width)
        value_blocks = value_piece[:whole].reshape(blocks, span, width)
        row_blocks = key_rows[:whole].reshape(blocks, span)

        def step_fn(carry, item):
            return (attend_block(carry, q_part, item[0], item[1], item[2]), None)

        state, _ = lax.scan(step_fn, state, (key_blocks, value_blocks, row_blocks))
        if whole < count:
            state = attend_block(state, q_part, key_piece[whole:], value_piece[whole:], key_rows[whole:])
        return state

    outer = lax.axis_size("c0")
    inner = lax.axis_size(INNER)
    rows_each = out_weight.shape[0]
    weight_rows = ring_all_gather(out_weight, "c0")
    half = kv_local // 2
    splits = [(0, half, ("c0", "c2", "c1")), (half, kv_local, ("c0", "c1", "c2"))]
    gathered, bounds = [], []
    for first, last, order in splits:
        if last == first:
            continue
        cols = slice(first * HEAD_WIDTH, last * HEAD_WIDTH)
        got, source = gather_order(jnp.concatenate([keys[:, cols], values[:, cols]], axis=1), order)
        key_rows = (source[:, None] * tok_dev + jnp.arange(tok_dev, dtype=jnp.int32)[None, :]).reshape(-1)
        gathered.append((got.reshape(n_ctx * tok_dev, -1), key_rows))
        bounds.append((first, last))
    gathered, weight_rows = lax.optimization_barrier((gathered, weight_rows))
    numerators, denominators = [], []
    for (first, last), (got, key_rows) in zip(bounds, gathered):
        width = (last - first) * HEAD_WIDTH
        numerator, denominator = attend(q_groups[:, first:last], got[:, :width], got[:, width:], key_rows)
        numerators.append(numerator)
        denominators.append(denominator)
    numerator = jnp.concatenate(numerators, axis=0)
    denominator = jnp.concatenate(denominators, axis=0)
    attended = (numerator / denominator[..., None]).astype(jnp.bfloat16)
    attended = attended.transpose(2, 0, 1, 3).reshape(tok_dev, kv_local * group_repeat * HEAD_WIDTH)
    all_heads = ring_all_gather(attended, "head").transpose(1, 0, 2).reshape(tok_dev, -1)
    weight_rows = weight_rows.reshape(outer * rows_each, out_weight.shape[1])
    blocks = all_heads.reshape(tok_dev, outer, inner, rows_each).transpose(2, 0, 1, 3)
    regrouped = permute_all_to_all(blocks, INNER)
    partial = jnp.dot(
        regrouped.reshape(inner * tok_dev, outer * rows_each), weight_rows, preferred_element_type=jnp.float32
    )
    mixed = permute_reduce_scatter(partial.reshape(inner, tok_dev, -1), INNER)
    squares = lax.psum(jnp.sum(mixed * mixed, axis=1), "head")
    normed = mixed / jnp.sqrt(squares / D + 1e-06)[:, None]
    out32 = hidden_in.astype(jnp.float32) + normed * out_gain[None, :]
    tok_reward = jnp.sum(out32 * reward_weight[None, :], axis=1)
    onehot = (query_doc[:, None] == jnp.arange(NDOC, dtype=jnp.int32)[None, :]).astype(jnp.float32)
    partial_sums = jnp.sum(onehot * tok_reward[:, None], axis=0)
    totals = butterfly_sum(partial_sums, CTX + ("head",))
    rewards = totals / jnp.sqrt(doc_lengths.astype(jnp.float32))
    return (out32.astype(jnp.bfloat16), rewards)


def solution(mesh):
    n_ctx, n_head = mesh.devices.shape
    split = Mesh(mesh.devices.reshape(n_ctx // 4, 2, 2, n_head), CTX + ("head",))
    rows = P(CTX, "head")
    in_specs = (rows, rows, rows, rows, rows, P("head"), P("head"), P())
    out_specs = (rows, P())
    return jax.shard_map(shards, mesh=split, in_specs=in_specs, out_specs=out_specs, check_vma=False)
```

```python
import jax
import jax.numpy as jnp
from jax import lax
from jax.sharding import Mesh, PartitionSpec as P

D = 4608
QUERY_HEADS = 32
KEY_VALUE_HEADS = 16
HEAD_WIDTH = 128
NDOC = 16


soft_cap = 50.0
CTX = ("c0", "c1", "c2")
INNER = ("c1", "c2")


def storage_positions(rows, tok_dev, n_ctx):
    owner = rows // tok_dev
    offset = rows % tok_dev
    half = tok_dev // 2
    slab = jnp.where(offset < half, owner, 2 * n_ctx - 1 - owner)
    return slab * half + offset % half


def document_of(positions, doc_ends):
    return jnp.sum((positions[:, None] >= doc_ends[None, :]).astype(jnp.int32), axis=1)


def ring_gather(x, axis):
    n = lax.axis_size(axis)
    pieces = [x]
    for _ in range(n - 1):
        pieces.append(lax.ppermute(pieces[-1], axis, [(k, (k + 1) % n) for k in range(n)]))
    return jnp.stack(pieces)


def gather_order(x, order):
    stride = {"c2": 1, "c1": lax.axis_size("c2"), "c0": lax.axis_size("c1") * lax.axis_size("c2")}
    source = jnp.zeros((), jnp.int32)
    for axis in order:
        x = ring_gather(x, axis)
        n = lax.axis_size(axis)
        came = (lax.axis_index(axis) - jnp.arange(n, dtype=jnp.int32)) % n
        source = came.reshape((n,) + (1,) * source.ndim) * stride[axis] + source[None]
    return x, source.reshape(-1)


def ring_all_gather(x, axis):
    n = lax.axis_size(axis)
    arrived = ring_gather(x, axis)[::-1]
    return jnp.roll(arrived, lax.axis_index(axis) + 1, axis=0)


def permute_all_to_all(x, axes):
    n = lax.axis_size(axes)
    own = lax.axis_index(axes)
    pieces = [lax.dynamic_index_in_dim(x, own, axis=0, keepdims=False)]
    for shift in range(1, n):
        sent = lax.dynamic_index_in_dim(x, (own + shift) % n, axis=0, keepdims=False)
        pieces.append(lax.ppermute(sent, axes, [(k, (k + shift) % n) for k in range(n)]))
    return jnp.roll(jnp.stack(pieces[::-1]), own + 1, axis=0)


def permute_reduce_scatter(x, axes):
    n = lax.axis_size(axes)
    own = lax.axis_index(axes)
    total = lax.dynamic_index_in_dim(x, own, axis=0, keepdims=False)
    for shift in range(1, n):
        sent = lax.dynamic_index_in_dim(x, (own + shift) % n, axis=0, keepdims=False)
        total = total + lax.ppermute(sent, axes, [(k, (k + shift) % n) for k in range(n)])
    return total


def butterfly_sum(x, axes):
    for axis in axes:
        size = lax.axis_size(axis)
        bit = 1
        while bit < size:
            x = x + lax.ppermute(x, axis, [(i, i ^ bit) for i in range(size)])
            bit *= 2
    return x


def shards(queries, keys, values, hidden_in, out_weight, out_gain, reward_weight, doc_lengths):
    n_ctx = lax.axis_size(CTX)
    device = lax.axis_index(CTX)
    tok_dev = queries.shape[0]
    kv_local = keys.shape[1] // HEAD_WIDTH
    group_repeat = QUERY_HEADS // KEY_VALUE_HEADS
    scale = (D / QUERY_HEADS) ** (-0.5)
    doc_ends = jnp.cumsum(doc_lengths)
    local_rows = device * tok_dev + jnp.arange(tok_dev, dtype=jnp.int32)
    query_pos = storage_positions(local_rows, tok_dev, n_ctx)
    query_doc = document_of(query_pos, doc_ends)
    q_groups = queries.reshape(tok_dev, kv_local, group_repeat, HEAD_WIDTH)
    span = tok_dev * max(1, 2048 // tok_dev)

    def attend_block(state, q_part, key_piece, value_piece, key_rows):
        count = key_piece.shape[0]
        heads = q_part.shape[1]
        key_pos = storage_positions(key_rows, tok_dev, n_ctx)
        key_doc = document_of(key_pos, doc_ends)
        visible = (query_doc[:, None] == key_doc[None, :]) & (
            key_pos[None, :] <= query_pos[:, None]
        )

        def compute(carry):
            numerator, denominator = carry
            scores = (
                jnp.einsum(
                    "qgrd,kgd->grqk",
                    q_part,
                    key_piece.reshape(count, heads, HEAD_WIDTH),
                    preferred_element_type=jnp.float32,
                )
                * scale
            )
            scores = soft_cap * jnp.tanh(scores / soft_cap)
            weights = jnp.where(visible[None, None], jnp.exp(scores), 0.0)
            numerator = numerator + jnp.einsum(
                "grqk,kgd->grqd",
                weights.astype(jnp.bfloat16),
                value_piece.reshape(count, heads, HEAD_WIDTH),
                preferred_element_type=jnp.float32,
            )
            denominator = denominator + jnp.sum(weights, axis=-1)
            return (numerator, denominator)

        if count == n_ctx * tok_dev:
            return compute(state)
        return lax.cond(jnp.any(visible), compute, lambda carry: carry, state)

    def attend(q_part, key_piece, value_piece, key_rows):
        heads = q_part.shape[1]
        state = (
            jnp.zeros((heads, group_repeat, tok_dev, HEAD_WIDTH), jnp.float32),
            jnp.zeros((heads, group_repeat, tok_dev), jnp.float32),
        )
        count = key_piece.shape[0]
        if count <= span:
            return attend_block(state, q_part, key_piece, value_piece, key_rows)
        blocks = count // span
        whole = blocks * span
        width = key_piece.shape[1]
        key_blocks = key_piece[:whole].reshape(blocks, span, width)
        value_blocks = value_piece[:whole].reshape(blocks, span, width)
        row_blocks = key_rows[:whole].reshape(blocks, span)

        def step_fn(carry, item):
            return (attend_block(carry, q_part, item[0], item[1], item[2]), None)

        state, _ = lax.scan(step_fn, state, (key_blocks, value_blocks, row_blocks))
        if whole < count:
            state = attend_block(state, q_part, key_piece[whole:], value_piece[whole:], key_rows[whole:])
        return state

    outer = lax.axis_size("c0")
    inner = lax.axis_size(INNER)
    rows_each = out_weight.shape[0]
    weight_rows = ring_gather(out_weight, "c0")
    arrival = (lax.axis_index("c0") - jnp.arange(outer, dtype=jnp.int32)) % outer
    half = kv_local // 2
    splits = [(0, half, ("c0", "c2", "c1")), (half, kv_local, ("c0", "c1", "c2"))]
    gathered, bounds = [], []
    for first, last, order in splits:
        if last == first:
            continue
        cols = slice(first * HEAD_WIDTH, last * HEAD_WIDTH)
        got, source = gather_order(jnp.concatenate([keys[:, cols], values[:, cols]], axis=1), order)
        key_rows = (source[:, None] * tok_dev + jnp.arange(tok_dev, dtype=jnp.int32)[None, :]).reshape(-1)
        gathered.append((got.reshape(n_ctx * tok_dev, -1), key_rows))
        bounds.append((first, last))
    gathered, weight_rows = lax.optimization_barrier((gathered, weight_rows))
    numerators, denominators = [], []
    for (first, last), (got, key_rows) in zip(bounds, gathered):
        width = (last - first) * HEAD_WIDTH
        numerator, denominator = attend(q_groups[:, first:last], got[:, :width], got[:, width:], key_rows)
        numerators.append(numerator)
        denominators.append(denominator)
    numerator = jnp.concatenate(numerators, axis=0)
    denominator = jnp.concatenate(denominators, axis=0)
    attended = (numerator / denominator[..., None]).astype(jnp.bfloat16)
    attended = attended.transpose(2, 0, 1, 3).reshape(tok_dev, kv_local * group_repeat * HEAD_WIDTH)
    all_heads = ring_all_gather(attended, "head").transpose(1, 0, 2).reshape(tok_dev, -1)
    weight_rows = weight_rows.reshape(outer * rows_each, out_weight.shape[1])
    blocks = all_heads.reshape(tok_dev, outer, inner, rows_each).transpose(2, 0, 1, 3)
    regrouped = permute_all_to_all(blocks, INNER)
    regrouped = jnp.take(regrouped.reshape(inner * tok_dev, outer, rows_each), arrival, axis=1)
    partial = jnp.dot(
        regrouped.reshape(inner * tok_dev, outer * rows_each), weight_rows, preferred_element_type=jnp.float32
    )
    mixed = permute_reduce_scatter(partial.reshape(inner, tok_dev, -1), INNER)
    squares = lax.psum(jnp.sum(mixed * mixed, axis=1), "head")
    normed = mixed / jnp.sqrt(squares / D + 1e-06)[:, None]
    out32 = hidden_in.astype(jnp.float32) + normed * out_gain[None, :]
    tok_reward = jnp.sum(out32 * reward_weight[None, :], axis=1)
    onehot = (query_doc[:, None] == jnp.arange(NDOC, dtype=jnp.int32)[None, :]).astype(jnp.float32)
    partial_sums = jnp.sum(onehot * tok_reward[:, None], axis=0)
    totals = butterfly_sum(partial_sums, CTX + ("head",))
    rewards = totals / jnp.sqrt(doc_lengths.astype(jnp.float32))
    return (out32.astype(jnp.bfloat16), rewards)


def solution(mesh):
    n_ctx, n_head = mesh.devices.shape
    split = Mesh(mesh.devices.reshape(n_ctx // 4, 2, 2, n_head), CTX + ("head",))
    rows = P(CTX, "head")
    in_specs = (rows, rows, rows, rows, rows, P("head"), P("head"), P())
    out_specs = (rows, P())
    return jax.shard_map(shards, mesh=split, in_specs=in_specs, out_specs=out_specs, check_vma=False)
```

```python
import jax
import jax.numpy as jnp
from jax import lax
from jax.sharding import Mesh, PartitionSpec as P

D = 4608
QUERY_HEADS = 32
KEY_VALUE_HEADS = 16
HEAD_WIDTH = 128
NDOC = 16


soft_cap = 50.0
CTX = ("c0", "c1", "c2")
INNER = ("c1", "c2")


def storage_positions(rows, tok_dev, n_ctx):
    owner = rows // tok_dev
    offset = rows % tok_dev
    half = tok_dev // 2
    slab = jnp.where(offset < half, owner, 2 * n_ctx - 1 - owner)
    return slab * half + offset % half


def document_of(positions, doc_ends):
    return jnp.sum((positions[:, None] >= doc_ends[None, :]).astype(jnp.int32), axis=1)


def ring_pieces(x, axis):
    n = lax.axis_size(axis)
    pieces = [x]
    for _ in range(n - 1):
        pieces.append(lax.ppermute(pieces[-1], axis, [(k, (k + 1) % n) for k in range(n)]))
    return pieces


def ring_gather(x, axis):
    return jnp.stack(ring_pieces(x, axis))


def gather_order(x, order):
    stride = {"c2": 1, "c1": lax.axis_size("c2"), "c0": lax.axis_size("c1") * lax.axis_size("c2")}
    source = jnp.zeros((), jnp.int32)
    for axis in order[:-1]:
        x = ring_gather(x, axis)
        n = lax.axis_size(axis)
        came = (lax.axis_index(axis) - jnp.arange(n, dtype=jnp.int32)) % n
        source = came.reshape((n,) + (1,) * source.ndim) * stride[axis] + source[None]
    last = order[-1]
    n = lax.axis_size(last)
    own = lax.axis_index(last)
    return [
        (piece, (((own - t) % n) * stride[last] + source).reshape(-1))
        for t, piece in enumerate(ring_pieces(x, last))
    ]


def ring_all_gather(x, axis):
    n = lax.axis_size(axis)
    arrived = ring_gather(x, axis)[::-1]
    return jnp.roll(arrived, lax.axis_index(axis) + 1, axis=0)


def permute_all_to_all(x, axes):
    n = lax.axis_size(axes)
    own = lax.axis_index(axes)
    pieces = [lax.dynamic_index_in_dim(x, own, axis=0, keepdims=False)]
    for shift in range(1, n):
        sent = lax.dynamic_index_in_dim(x, (own + shift) % n, axis=0, keepdims=False)
        pieces.append(lax.ppermute(sent, axes, [(k, (k + shift) % n) for k in range(n)]))
    return jnp.roll(jnp.stack(pieces[::-1]), own + 1, axis=0)


def permute_reduce_scatter(x, axes):
    n = lax.axis_size(axes)
    own = lax.axis_index(axes)
    total = lax.dynamic_index_in_dim(x, own, axis=0, keepdims=False)
    for shift in range(1, n):
        sent = lax.dynamic_index_in_dim(x, (own + shift) % n, axis=0, keepdims=False)
        total = total + lax.ppermute(sent, axes, [(k, (k + shift) % n) for k in range(n)])
    return total


def butterfly_sum(x, axes):
    for axis in axes:
        size = lax.axis_size(axis)
        bit = 1
        while bit < size:
            x = x + lax.ppermute(x, axis, [(i, i ^ bit) for i in range(size)])
            bit *= 2
    return x


def shards(queries, keys, values, hidden_in, out_weight, out_gain, reward_weight, doc_lengths):
    n_ctx = lax.axis_size(CTX)
    device = lax.axis_index(CTX)
    tok_dev = queries.shape[0]
    kv_local = keys.shape[1] // HEAD_WIDTH
    group_repeat = QUERY_HEADS // KEY_VALUE_HEADS
    scale = (D / QUERY_HEADS) ** (-0.5)
    doc_ends = jnp.cumsum(doc_lengths)
    local_rows = device * tok_dev + jnp.arange(tok_dev, dtype=jnp.int32)
    query_pos = storage_positions(local_rows, tok_dev, n_ctx)
    query_doc = document_of(query_pos, doc_ends)
    q_groups = queries.reshape(tok_dev, kv_local, group_repeat, HEAD_WIDTH)
    span = tok_dev * max(1, 2048 // tok_dev)

    def attend_block(state, q_part, key_piece, value_piece, key_rows):
        count = key_piece.shape[0]
        heads = q_part.shape[1]
        key_pos = storage_positions(key_rows, tok_dev, n_ctx)
        key_doc = document_of(key_pos, doc_ends)
        visible = (query_doc[:, None] == key_doc[None, :]) & (
            key_pos[None, :] <= query_pos[:, None]
        )

        def compute(carry):
            numerator, denominator = carry
            scores = (
                jnp.einsum(
                    "qgrd,kgd->grqk",
                    q_part,
                    key_piece.reshape(count, heads, HEAD_WIDTH),
                    preferred_element_type=jnp.float32,
                )
                * scale
            )
            scores = soft_cap * jnp.tanh(scores / soft_cap)
            weights = jnp.where(visible[None, None], jnp.exp(scores), 0.0)
            numerator = numerator + jnp.einsum(
                "grqk,kgd->grqd",
                weights.astype(jnp.bfloat16),
                value_piece.reshape(count, heads, HEAD_WIDTH),
                preferred_element_type=jnp.float32,
            )
            denominator = denominator + jnp.sum(weights, axis=-1)
            return (numerator, denominator)

        if count <= span:
            return compute(state)
        return lax.cond(jnp.any(visible), compute, lambda carry: carry, state)

    def attend(state, q_part, key_piece, value_piece, key_rows):
        count = key_piece.shape[0]
        if count <= span:
            return attend_block(state, q_part, key_piece, value_piece, key_rows)
        blocks = count // span
        whole = blocks * span
        width = key_piece.shape[1]
        key_blocks = key_piece[:whole].reshape(blocks, span, width)
        value_blocks = value_piece[:whole].reshape(blocks, span, width)
        row_blocks = key_rows[:whole].reshape(blocks, span)

        def step_fn(carry, item):
            return (attend_block(carry, q_part, item[0], item[1], item[2]), None)

        state, _ = lax.scan(step_fn, state, (key_blocks, value_blocks, row_blocks))
        if whole < count:
            state = attend_block(state, q_part, key_piece[whole:], value_piece[whole:], key_rows[whole:])
        return state

    outer = lax.axis_size("c0")
    inner = lax.axis_size(INNER)
    rows_each = out_weight.shape[0]
    weight_rows = ring_gather(out_weight, "c0")
    arrival = (lax.axis_index("c0") - jnp.arange(outer, dtype=jnp.int32)) % outer
    half = kv_local // 2
    splits = [(0, half, ("c0", "c2", "c1")), (half, kv_local, ("c0", "c1", "c2"))]
    gathered, bounds = [], []
    for first, last, order in splits:
        if last == first:
            continue
        cols = slice(first * HEAD_WIDTH, last * HEAD_WIDTH)
        for got, source in gather_order(jnp.concatenate([keys[:, cols], values[:, cols]], axis=1), order):
            key_rows = (source[:, None] * tok_dev + jnp.arange(tok_dev, dtype=jnp.int32)[None, :]).reshape(-1)
            gathered.append((got.reshape(key_rows.shape[0], -1), key_rows))
            bounds.append((first, last))
    gathered, weight_rows = lax.optimization_barrier((gathered, weight_rows))
    numerators, denominators = [], []
    states = {}
    for (first, last), (got, key_rows) in zip(bounds, gathered):
        width = (last - first) * HEAD_WIDTH
        q_part = q_groups[:, first:last]
        state = states.get((first, last), (
            jnp.zeros((last - first, group_repeat, tok_dev, HEAD_WIDTH), jnp.float32),
            jnp.zeros((last - first, group_repeat, tok_dev), jnp.float32),
        ))
        states[(first, last)] = attend(state, q_part, got[:, :width], got[:, width:], key_rows)
    for key in sorted(states):
        numerators.append(states[key][0])
        denominators.append(states[key][1])
    numerator = jnp.concatenate(numerators, axis=0)
    denominator = jnp.concatenate(denominators, axis=0)
    attended = (numerator / denominator[..., None]).astype(jnp.bfloat16)
    attended = attended.transpose(2, 0, 1, 3).reshape(tok_dev, kv_local * group_repeat * HEAD_WIDTH)
    all_heads = ring_all_gather(attended, "head").transpose(1, 0, 2).reshape(tok_dev, -1)
    weight_rows = weight_rows.reshape(outer * rows_each, out_weight.shape[1])
    blocks = all_heads.reshape(tok_dev, outer, inner, rows_each).transpose(2, 0, 1, 3)
    regrouped = permute_all_to_all(blocks, INNER)
    regrouped = jnp.take(regrouped.reshape(inner * tok_dev, outer, rows_each), arrival, axis=1)
    partial = jnp.dot(
        regrouped.reshape(inner * tok_dev, outer * rows_each), weight_rows, preferred_element_type=jnp.float32
    )
    mixed = permute_reduce_scatter(partial.reshape(inner, tok_dev, -1), INNER)
    squares = lax.psum(jnp.sum(mixed * mixed, axis=1), "head")
    normed = mixed / jnp.sqrt(squares / D + 1e-06)[:, None]
    out32 = hidden_in.astype(jnp.float32) + normed * out_gain[None, :]
    tok_reward = jnp.sum(out32 * reward_weight[None, :], axis=1)
    onehot = (query_doc[:, None] == jnp.arange(NDOC, dtype=jnp.int32)[None, :]).astype(jnp.float32)
    partial_sums = jnp.sum(onehot * tok_reward[:, None], axis=0)
    totals = butterfly_sum(partial_sums, CTX + ("head",))
    rewards = totals / jnp.sqrt(doc_lengths.astype(jnp.float32))
    return (out32.astype(jnp.bfloat16), rewards)


def solution(mesh):
    n_ctx, n_head = mesh.devices.shape
    split = Mesh(mesh.devices.reshape(n_ctx // 4, 2, 2, n_head), CTX + ("head",))
    rows = P(CTX, "head")
    in_specs = (rows, rows, rows, rows, rows, P("head"), P("head"), P())
    out_specs = (rows, P())
    return jax.shard_map(shards, mesh=split, in_specs=in_specs, out_specs=out_specs, check_vma=False)
```

```python
import jax
import jax.numpy as jnp
from jax import lax
from jax.sharding import Mesh, PartitionSpec as P

D = 4608
QUERY_HEADS = 32
KEY_VALUE_HEADS = 16
HEAD_WIDTH = 128
NDOC = 16


soft_cap = 50.0
CTX = ("c0", "c1", "c2")
INNER = ("c1", "c2")


def storage_positions(rows, tok_dev, n_ctx):
    owner = rows // tok_dev
    offset = rows % tok_dev
    half = tok_dev // 2
    slab = jnp.where(offset < half, owner, 2 * n_ctx - 1 - owner)
    return slab * half + offset % half


def document_of(positions, doc_ends):
    return jnp.sum((positions[:, None] >= doc_ends[None, :]).astype(jnp.int32), axis=1)


def ring_pieces(x, axis):
    n = lax.axis_size(axis)
    pieces = [x]
    for _ in range(n - 1):
        pieces.append(lax.ppermute(pieces[-1], axis, [(k, (k + 1) % n) for k in range(n)]))
    return pieces


def ring_gather(x, axis):
    return jnp.stack(ring_pieces(x, axis))


def gather_order(x, order):
    stride = {"c2": 1, "c1": lax.axis_size("c2"), "c0": lax.axis_size("c1") * lax.axis_size("c2")}
    source = jnp.zeros((), jnp.int32)
    for axis in order[:-1]:
        x = ring_gather(x, axis)
        n = lax.axis_size(axis)
        came = (lax.axis_index(axis) - jnp.arange(n, dtype=jnp.int32)) % n
        source = came.reshape((n,) + (1,) * source.ndim) * stride[axis] + source[None]
    last = order[-1]
    n = lax.axis_size(last)
    own = lax.axis_index(last)
    return [
        (piece, (((own - t) % n) * stride[last] + source).reshape(-1))
        for t, piece in enumerate(ring_pieces(x, last))
    ]


def ring_all_gather(x, axis):
    n = lax.axis_size(axis)
    arrived = ring_gather(x, axis)[::-1]
    return jnp.roll(arrived, lax.axis_index(axis) + 1, axis=0)


def permute_all_to_all(x, axes):
    n = lax.axis_size(axes)
    own = lax.axis_index(axes)
    pieces = [lax.dynamic_index_in_dim(x, own, axis=0, keepdims=False)]
    for shift in range(1, n):
        sent = lax.dynamic_index_in_dim(x, (own + shift) % n, axis=0, keepdims=False)
        pieces.append(lax.ppermute(sent, axes, [(k, (k + shift) % n) for k in range(n)]))
    return jnp.roll(jnp.stack(pieces[::-1]), own + 1, axis=0)


def permute_reduce_scatter(x, axes):
    n = lax.axis_size(axes)
    own = lax.axis_index(axes)
    total = lax.dynamic_index_in_dim(x, own, axis=0, keepdims=False)
    for shift in range(1, n):
        sent = lax.dynamic_index_in_dim(x, (own + shift) % n, axis=0, keepdims=False)
        total = total + lax.ppermute(sent, axes, [(k, (k + shift) % n) for k in range(n)])
    return total


def butterfly_sum(x, axes):
    for axis in axes:
        size = lax.axis_size(axis)
        bit = 1
        while bit < size:
            x = x + lax.ppermute(x, axis, [(i, i ^ bit) for i in range(size)])
            bit *= 2
    return x


def shards(queries, keys, values, hidden_in, out_weight, out_gain, reward_weight, doc_lengths):
    n_ctx = lax.axis_size(CTX)
    device = lax.axis_index(CTX)
    tok_dev = queries.shape[0]
    kv_local = keys.shape[1] // HEAD_WIDTH
    group_repeat = QUERY_HEADS // KEY_VALUE_HEADS
    scale = (D / QUERY_HEADS) ** (-0.5)
    doc_ends = jnp.cumsum(doc_lengths)
    local_rows = device * tok_dev + jnp.arange(tok_dev, dtype=jnp.int32)
    query_pos = storage_positions(local_rows, tok_dev, n_ctx)
    query_doc = document_of(query_pos, doc_ends)
    q_groups = queries.reshape(tok_dev, kv_local, group_repeat, HEAD_WIDTH)
    span = tok_dev * max(1, 2048 // tok_dev)

    def attend_block(state, q_part, key_piece, value_piece, key_rows):
        count = key_piece.shape[0]
        heads = q_part.shape[1]
        key_pos = storage_positions(key_rows, tok_dev, n_ctx)
        key_doc = document_of(key_pos, doc_ends)
        visible = (query_doc[:, None] == key_doc[None, :]) & (
            key_pos[None, :] <= query_pos[:, None]
        )

        def compute(carry):
            numerator, denominator = carry
            scores = (
                jnp.einsum(
                    "qgrd,kgd->grqk",
                    q_part,
                    key_piece.reshape(count, heads, HEAD_WIDTH),
                    preferred_element_type=jnp.float32,
                )
                * scale
            )
            scores = soft_cap * jnp.tanh(scores / soft_cap)
            weights = jnp.where(visible[None, None], jnp.exp(scores), 0.0)
            numerator = numerator + jnp.einsum(
                "grqk,kgd->grqd",
                weights.astype(jnp.bfloat16),
                value_piece.reshape(count, heads, HEAD_WIDTH),
                preferred_element_type=jnp.float32,
            )
            denominator = denominator + jnp.sum(weights, axis=-1)
            return (numerator, denominator)

        if count <= span:
            return compute(state)
        return lax.cond(jnp.any(visible), compute, lambda carry: carry, state)

    def attend(state, q_part, key_piece, value_piece, key_rows):
        count = key_piece.shape[0]
        if count <= span:
            return attend_block(state, q_part, key_piece, value_piece, key_rows)
        blocks = count // span
        whole = blocks * span
        width = key_piece.shape[1]
        key_blocks = key_piece[:whole].reshape(blocks, span, width)
        value_blocks = value_piece[:whole].reshape(blocks, span, width)
        row_blocks = key_rows[:whole].reshape(blocks, span)

        def step_fn(carry, item):
            return (attend_block(carry, q_part, item[0], item[1], item[2]), None)

        state, _ = lax.scan(step_fn, state, (key_blocks, value_blocks, row_blocks))
        if whole < count:
            state = attend_block(state, q_part, key_piece[whole:], value_piece[whole:], key_rows[whole:])
        return state

    outer = lax.axis_size("c0")
    inner = lax.axis_size(INNER)
    rows_each = out_weight.shape[0]
    weight_rows = ring_gather(out_weight, "c0")
    arrival = (lax.axis_index("c0") - jnp.arange(outer, dtype=jnp.int32)) % outer
    half = kv_local // 2
    splits = [(0, half, ("c0", "c2", "c1")), (half, kv_local, ("c0", "c1", "c2"))]
    gathered, bounds = [], []
    for first, last, order in splits:
        if last == first:
            continue
        cols = slice(first * HEAD_WIDTH, last * HEAD_WIDTH)
        for got, source in gather_order(jnp.concatenate([keys[:, cols], values[:, cols]], axis=1), order):
            key_rows = (source[:, None] * tok_dev + jnp.arange(tok_dev, dtype=jnp.int32)[None, :]).reshape(-1)
            gathered.append((got.reshape(key_rows.shape[0], -1), key_rows))
            bounds.append((first, last))
    gathered, weight_rows = lax.optimization_barrier((gathered, weight_rows))
    numerators, denominators = [], []
    states = {}
    for (first, last), (got, key_rows) in zip(bounds, gathered):
        width = (last - first) * HEAD_WIDTH
        q_part = q_groups[:, first:last]
        state = states.get((first, last), (
            jnp.zeros((last - first, group_repeat, tok_dev, HEAD_WIDTH), jnp.float32),
            jnp.zeros((last - first, group_repeat, tok_dev), jnp.float32),
        ))
        states[(first, last)] = attend(state, q_part, got[:, :width], got[:, width:], key_rows)
    for key in sorted(states):
        numerators.append(states[key][0])
        denominators.append(states[key][1])
    numerator = jnp.concatenate(numerators, axis=0)
    denominator = jnp.concatenate(denominators, axis=0)
    attended = (numerator / denominator[..., None]).astype(jnp.bfloat16)
    attended = attended.transpose(2, 0, 1, 3).reshape(tok_dev, kv_local * group_repeat * HEAD_WIDTH)
    all_heads = ring_all_gather(attended, "head").transpose(1, 0, 2).reshape(tok_dev, -1)
    weight_rows = weight_rows.reshape(outer * rows_each, out_weight.shape[1])
    blocks = all_heads.reshape(tok_dev, outer, inner, rows_each).transpose(2, 0, 1, 3)
    regrouped = permute_all_to_all(blocks, INNER)
    regrouped = jnp.take(regrouped.reshape(inner * tok_dev, outer, rows_each), arrival, axis=1)
    partial = jnp.dot(
        regrouped.reshape(inner * tok_dev, outer * rows_each), weight_rows, preferred_element_type=jnp.float32
    )
    mixed = permute_reduce_scatter(partial.reshape(inner, tok_dev, -1), INNER)
    hidden = hidden_in.astype(jnp.float32)
    sums = lax.psum(
        jnp.stack([
            jnp.sum(mixed * mixed, axis=1),
            jnp.sum(hidden * reward_weight[None, :], axis=1),
            jnp.sum(mixed * (out_gain * reward_weight)[None, :], axis=1),
        ]),
        "head",
    )
    rms = jnp.sqrt(sums[0] / D + 1e-06)
    normed = mixed / rms[:, None]
    out32 = hidden + normed * out_gain[None, :]
    tok_reward = sums[1] + sums[2] / rms
    onehot = (query_doc[:, None] == jnp.arange(NDOC, dtype=jnp.int32)[None, :]).astype(jnp.float32)
    partial_sums = jnp.sum(onehot * tok_reward[:, None], axis=0)
    totals = butterfly_sum(partial_sums, CTX)
    rewards = totals / jnp.sqrt(doc_lengths.astype(jnp.float32))
    return (out32.astype(jnp.bfloat16), rewards)


def solution(mesh):
    n_ctx, n_head = mesh.devices.shape
    split = Mesh(mesh.devices.reshape(n_ctx // 4, 2, 2, n_head), CTX + ("head",))
    rows = P(CTX, "head")
    in_specs = (rows, rows, rows, rows, rows, P("head"), P("head"), P())
    out_specs = (rows, P())
    return jax.shard_map(shards, mesh=split, in_specs=in_specs, out_specs=out_specs, check_vma=False)
```

```python
import jax
import jax.numpy as jnp
from jax import lax
from jax.sharding import Mesh, PartitionSpec as P

D = 4608
QUERY_HEADS = 32
KEY_VALUE_HEADS = 16
HEAD_WIDTH = 128
NDOC = 16


soft_cap = 50.0
CTX = ("c0", "c1", "c2")
INNER = ("c1", "c2")


def storage_positions(rows, tok_dev, n_ctx):
    owner = rows // tok_dev
    offset = rows % tok_dev
    half = tok_dev // 2
    slab = jnp.where(offset < half, owner, 2 * n_ctx - 1 - owner)
    return slab * half + offset % half


def document_of(positions, doc_ends):
    return jnp.sum((positions[:, None] >= doc_ends[None, :]).astype(jnp.int32), axis=1)


def ring_pieces(x, axis):
    n = lax.axis_size(axis)
    pieces = [x]
    for _ in range(n - 1):
        pieces.append(lax.ppermute(pieces[-1], axis, [(k, (k + 1) % n) for k in range(n)]))
    return pieces


def ring_gather(x, axis):
    return jnp.stack(ring_pieces(x, axis))


def gather_order(x, order):
    stride = {"c2": 1, "c1": lax.axis_size("c2"), "c0": lax.axis_size("c1") * lax.axis_size("c2")}
    source = jnp.zeros((), jnp.int32)
    for axis in order[:-1]:
        x = ring_gather(x, axis)
        n = lax.axis_size(axis)
        came = (lax.axis_index(axis) - jnp.arange(n, dtype=jnp.int32)) % n
        source = came.reshape((n,) + (1,) * source.ndim) * stride[axis] + source[None]
    last = order[-1]
    n = lax.axis_size(last)
    own = lax.axis_index(last)
    return [
        (piece, (((own - t) % n) * stride[last] + source).reshape(-1))
        for t, piece in enumerate(ring_pieces(x, last))
    ]


def ring_all_gather(x, axis):
    n = lax.axis_size(axis)
    arrived = ring_gather(x, axis)[::-1]
    return jnp.roll(arrived, lax.axis_index(axis) + 1, axis=0)


def permute_all_to_all(x, axes):
    n = lax.axis_size(axes)
    own = lax.axis_index(axes)
    pieces = [lax.dynamic_index_in_dim(x, own, axis=0, keepdims=False)]
    for shift in range(1, n):
        sent = lax.dynamic_index_in_dim(x, (own + shift) % n, axis=0, keepdims=False)
        pieces.append(lax.ppermute(sent, axes, [(k, (k + shift) % n) for k in range(n)]))
    return jnp.roll(jnp.stack(pieces[::-1]), own + 1, axis=0)


def permute_reduce_scatter(x, axes):
    n = lax.axis_size(axes)
    own = lax.axis_index(axes)
    total = lax.dynamic_index_in_dim(x, own, axis=0, keepdims=False)
    for shift in range(1, n):
        sent = lax.dynamic_index_in_dim(x, (own + shift) % n, axis=0, keepdims=False)
        total = total + lax.ppermute(sent, axes, [(k, (k + shift) % n) for k in range(n)])
    return total


def swap_reduce_scatter(x, first, second):
    own_first = lax.axis_index(first)
    own_second = lax.axis_index(second)
    keep = lax.dynamic_index_in_dim(x, own_first, axis=1, keepdims=False)
    sent = lax.dynamic_index_in_dim(x, 1 - own_first, axis=1, keepdims=False)
    keep = keep + lax.ppermute(sent, first, [(0, 1), (1, 0)])
    mine = lax.dynamic_index_in_dim(keep, own_second, axis=0, keepdims=False)
    sent = lax.dynamic_index_in_dim(keep, 1 - own_second, axis=0, keepdims=False)
    return mine + lax.ppermute(sent, second, [(0, 1), (1, 0)])


def butterfly_sum(x, axes):
    for axis in axes:
        size = lax.axis_size(axis)
        bit = 1
        while bit < size:
            x = x + lax.ppermute(x, axis, [(i, i ^ bit) for i in range(size)])
            bit *= 2
    return x


def shards(queries, keys, values, hidden_in, out_weight, out_gain, reward_weight, doc_lengths):
    n_ctx = lax.axis_size(CTX)
    device = lax.axis_index(CTX)
    tok_dev = queries.shape[0]
    kv_local = keys.shape[1] // HEAD_WIDTH
    group_repeat = QUERY_HEADS // KEY_VALUE_HEADS
    scale = (D / QUERY_HEADS) ** (-0.5)
    doc_ends = jnp.cumsum(doc_lengths)
    local_rows = device * tok_dev + jnp.arange(tok_dev, dtype=jnp.int32)
    query_pos = storage_positions(local_rows, tok_dev, n_ctx)
    query_doc = document_of(query_pos, doc_ends)
    q_groups = queries.reshape(tok_dev, kv_local, group_repeat, HEAD_WIDTH)
    span = tok_dev * max(1, 2048 // tok_dev)

    def attend_block(state, q_part, key_piece, value_piece, key_rows):
        count = key_piece.shape[0]
        heads = q_part.shape[1]
        key_pos = storage_positions(key_rows, tok_dev, n_ctx)
        key_doc = document_of(key_pos, doc_ends)
        visible = (query_doc[:, None] == key_doc[None, :]) & (
            key_pos[None, :] <= query_pos[:, None]
        )

        def compute(carry):
            numerator, denominator = carry
            scores = (
                jnp.einsum(
                    "qgrd,kgd->grqk",
                    q_part,
                    key_piece.reshape(count, heads, HEAD_WIDTH),
                    preferred_element_type=jnp.float32,
                )
                * scale
            )
            scores = soft_cap * jnp.tanh(scores / soft_cap)
            weights = jnp.where(visible[None, None], jnp.exp(scores), 0.0)
            numerator = numerator + jnp.einsum(
                "grqk,kgd->grqd",
                weights.astype(jnp.bfloat16),
                value_piece.reshape(count, heads, HEAD_WIDTH),
                preferred_element_type=jnp.float32,
            )
            denominator = denominator + jnp.sum(weights, axis=-1)
            return (numerator, denominator)

        if count <= span:
            return compute(state)
        return lax.cond(jnp.any(visible), compute, lambda carry: carry, state)

    def attend(state, q_part, key_piece, value_piece, key_rows):
        count = key_piece.shape[0]
        if count <= span:
            return attend_block(state, q_part, key_piece, value_piece, key_rows)
        blocks = count // span
        whole = blocks * span
        width = key_piece.shape[1]
        key_blocks = key_piece[:whole].reshape(blocks, span, width)
        value_blocks = value_piece[:whole].reshape(blocks, span, width)
        row_blocks = key_rows[:whole].reshape(blocks, span)

        def step_fn(carry, item):
            return (attend_block(carry, q_part, item[0], item[1], item[2]), None)

        state, _ = lax.scan(step_fn, state, (key_blocks, value_blocks, row_blocks))
        if whole < count:
            state = attend_block(state, q_part, key_piece[whole:], value_piece[whole:], key_rows[whole:])
        return state

    outer = lax.axis_size("c0")
    inner = lax.axis_size(INNER)
    rows_each = out_weight.shape[0]
    weight_rows = ring_gather(out_weight, "c0")
    arrival = (lax.axis_index("c0") - jnp.arange(outer, dtype=jnp.int32)) % outer
    half = kv_local // 2
    splits = [(0, half, ("c0", "c2", "c1")), (half, kv_local, ("c0", "c1", "c2"))]
    gathered, bounds = [], []
    for first, last, order in splits:
        if last == first:
            continue
        cols = slice(first * HEAD_WIDTH, last * HEAD_WIDTH)
        for got, source in gather_order(jnp.concatenate([keys[:, cols], values[:, cols]], axis=1), order):
            key_rows = (source[:, None] * tok_dev + jnp.arange(tok_dev, dtype=jnp.int32)[None, :]).reshape(-1)
            gathered.append((got.reshape(key_rows.shape[0], -1), key_rows))
            bounds.append((first, last))
    gathered, weight_rows = lax.optimization_barrier((gathered, weight_rows))
    numerators, denominators = [], []
    states = {}
    for (first, last), (got, key_rows) in zip(bounds, gathered):
        width = (last - first) * HEAD_WIDTH
        q_part = q_groups[:, first:last]
        state = states.get((first, last), (
            jnp.zeros((last - first, group_repeat, tok_dev, HEAD_WIDTH), jnp.float32),
            jnp.zeros((last - first, group_repeat, tok_dev), jnp.float32),
        ))
        states[(first, last)] = attend(state, q_part, got[:, :width], got[:, width:], key_rows)
    for key in sorted(states):
        numerators.append(states[key][0])
        denominators.append(states[key][1])
    numerator = jnp.concatenate(numerators, axis=0)
    denominator = jnp.concatenate(denominators, axis=0)
    attended = (numerator / denominator[..., None]).astype(jnp.bfloat16)
    attended = attended.transpose(2, 0, 1, 3).reshape(tok_dev, kv_local * group_repeat * HEAD_WIDTH)
    all_heads = ring_all_gather(attended, "head").transpose(1, 0, 2).reshape(tok_dev, -1)
    weight_rows = weight_rows.reshape(outer * rows_each, out_weight.shape[1])
    blocks = all_heads.reshape(tok_dev, outer, inner, rows_each).transpose(2, 0, 1, 3)
    regrouped = permute_all_to_all(blocks, INNER)
    regrouped = jnp.take(regrouped.reshape(inner * tok_dev, outer, rows_each), arrival, axis=1)
    partial = jnp.dot(
        regrouped.reshape(inner * tok_dev, outer * rows_each), weight_rows, preferred_element_type=jnp.float32
    )
    by_dest = partial.reshape(2, 2, tok_dev, -1)
    cut = by_dest.shape[-1] // 2
    mixed = jnp.concatenate([
        swap_reduce_scatter(by_dest[..., :cut], "c2", "c1"),
        swap_reduce_scatter(by_dest[..., cut:].transpose(1, 0, 2, 3), "c1", "c2"),
    ], axis=-1)
    hidden = hidden_in.astype(jnp.float32)
    sums = lax.psum(
        jnp.stack([
            jnp.sum(mixed * mixed, axis=1),
            jnp.sum(hidden * reward_weight[None, :], axis=1),
            jnp.sum(mixed * (out_gain * reward_weight)[None, :], axis=1),
        ]),
        "head",
    )
    rms = jnp.sqrt(sums[0] / D + 1e-06)
    normed = mixed / rms[:, None]
    out32 = hidden + normed * out_gain[None, :]
    tok_reward = sums[1] + sums[2] / rms
    onehot = (query_doc[:, None] == jnp.arange(NDOC, dtype=jnp.int32)[None, :]).astype(jnp.float32)
    partial_sums = jnp.sum(onehot * tok_reward[:, None], axis=0)
    totals = butterfly_sum(partial_sums, CTX)
    rewards = totals / jnp.sqrt(doc_lengths.astype(jnp.float32))
    return (out32.astype(jnp.bfloat16), rewards)


def solution(mesh):
    n_ctx, n_head = mesh.devices.shape
    split = Mesh(mesh.devices.reshape(n_ctx // 4, 2, 2, n_head), CTX + ("head",))
    rows = P(CTX, "head")
    in_specs = (rows, rows, rows, rows, rows, P("head"), P("head"), P())
    out_specs = (rows, P())
    return jax.shard_map(shards, mesh=split, in_specs=in_specs, out_specs=out_specs, check_vma=False)
```

```python
import jax
import jax.numpy as jnp
from jax import lax
from jax.sharding import Mesh, PartitionSpec as P

D = 4608
QUERY_HEADS = 32
KEY_VALUE_HEADS = 16
HEAD_WIDTH = 128
NDOC = 16


soft_cap = 50.0
CTX = ("c0", "c1", "c2")
INNER = ("c1", "c2")


def storage_positions(rows, tok_dev, n_ctx):
    owner = rows // tok_dev
    offset = rows % tok_dev
    half = tok_dev // 2
    slab = jnp.where(offset < half, owner, 2 * n_ctx - 1 - owner)
    return slab * half + offset % half


def document_of(positions, doc_ends):
    return jnp.sum((positions[:, None] >= doc_ends[None, :]).astype(jnp.int32), axis=1)


def ring_pieces(x, axis):
    n = lax.axis_size(axis)
    pieces = [x]
    for _ in range(n - 1):
        pieces.append(lax.ppermute(pieces[-1], axis, [(k, (k + 1) % n) for k in range(n)]))
    return pieces


def ring_gather(x, axis):
    return jnp.stack(ring_pieces(x, axis))


def gather_order(x, order):
    stride = {"c2": 1, "c1": lax.axis_size("c2"), "c0": lax.axis_size("c1") * lax.axis_size("c2")}
    source = jnp.zeros((), jnp.int32)
    for axis in order[:-1]:
        x = ring_gather(x, axis)
        n = lax.axis_size(axis)
        came = (lax.axis_index(axis) - jnp.arange(n, dtype=jnp.int32)) % n
        source = came.reshape((n,) + (1,) * source.ndim) * stride[axis] + source[None]
    last = order[-1]
    n = lax.axis_size(last)
    own = lax.axis_index(last)
    return [
        (piece, (((own - t) % n) * stride[last] + source).reshape(-1))
        for t, piece in enumerate(ring_pieces(x, last))
    ]


def ring_all_gather(x, axis):
    n = lax.axis_size(axis)
    arrived = ring_gather(x, axis)[::-1]
    return jnp.roll(arrived, lax.axis_index(axis) + 1, axis=0)


def permute_all_to_all(x, axes):
    n = lax.axis_size(axes)
    own = lax.axis_index(axes)
    pieces = [lax.dynamic_index_in_dim(x, own, axis=0, keepdims=False)]
    for shift in range(1, n):
        sent = lax.dynamic_index_in_dim(x, (own + shift) % n, axis=0, keepdims=False)
        pieces.append(lax.ppermute(sent, axes, [(k, (k + shift) % n) for k in range(n)]))
    return jnp.roll(jnp.stack(pieces[::-1]), own + 1, axis=0)


def permute_reduce_scatter(x, axes):
    n = lax.axis_size(axes)
    own = lax.axis_index(axes)
    total = lax.dynamic_index_in_dim(x, own, axis=0, keepdims=False)
    for shift in range(1, n):
        sent = lax.dynamic_index_in_dim(x, (own + shift) % n, axis=0, keepdims=False)
        total = total + lax.ppermute(sent, axes, [(k, (k + shift) % n) for k in range(n)])
    return total


def swap_reduce_scatter(x, first, second):
    own_first = lax.axis_index(first)
    own_second = lax.axis_index(second)
    keep = lax.dynamic_index_in_dim(x, own_first, axis=1, keepdims=False)
    sent = lax.dynamic_index_in_dim(x, 1 - own_first, axis=1, keepdims=False)
    keep = keep + lax.ppermute(sent, first, [(0, 1), (1, 0)])
    mine = lax.dynamic_index_in_dim(keep, own_second, axis=0, keepdims=False)
    sent = lax.dynamic_index_in_dim(keep, 1 - own_second, axis=0, keepdims=False)
    return mine + lax.ppermute(sent, second, [(0, 1), (1, 0)])


def butterfly_sum(x, axes):
    for axis in axes:
        size = lax.axis_size(axis)
        bit = 1
        while bit < size:
            x = x + lax.ppermute(x, axis, [(i, i ^ bit) for i in range(size)])
            bit *= 2
    return x


def shards(queries, keys, values, hidden_in, out_weight, out_gain, reward_weight, doc_lengths):
    n_ctx = lax.axis_size(CTX)
    device = lax.axis_index(CTX)
    tok_dev = queries.shape[0]
    kv_local = keys.shape[1] // HEAD_WIDTH
    group_repeat = QUERY_HEADS // KEY_VALUE_HEADS
    scale = (D / QUERY_HEADS) ** (-0.5)
    doc_ends = jnp.cumsum(doc_lengths)
    local_rows = device * tok_dev + jnp.arange(tok_dev, dtype=jnp.int32)
    query_pos = storage_positions(local_rows, tok_dev, n_ctx)
    query_doc = document_of(query_pos, doc_ends)
    q_groups = queries.reshape(tok_dev, kv_local, group_repeat, HEAD_WIDTH)
    span = tok_dev * max(1, 2048 // tok_dev)

    def attend_block(state, q_part, key_piece, value_piece, key_rows):
        count = key_piece.shape[0]
        heads = q_part.shape[1]
        key_pos = storage_positions(key_rows, tok_dev, n_ctx)
        key_doc = document_of(key_pos, doc_ends)
        visible = (query_doc[:, None] == key_doc[None, :]) & (
            key_pos[None, :] <= query_pos[:, None]
        )

        def compute(carry):
            numerator, denominator = carry
            scores = (
                jnp.einsum(
                    "qgrd,kgd->grqk",
                    q_part,
                    key_piece.reshape(count, heads, HEAD_WIDTH),
                    preferred_element_type=jnp.float32,
                )
                * scale
            )
            scores = soft_cap * jnp.tanh(scores / soft_cap)
            weights = jnp.where(visible[None, None], jnp.exp(scores), 0.0)
            numerator = numerator + jnp.einsum(
                "grqk,kgd->grqd",
                weights.astype(jnp.bfloat16),
                value_piece.reshape(count, heads, HEAD_WIDTH),
                preferred_element_type=jnp.float32,
            )
            denominator = denominator + jnp.sum(weights, axis=-1)
            return (numerator, denominator)

        if count <= span:
            return compute(state)
        return lax.cond(jnp.any(visible), compute, lambda carry: carry, state)

    def attend(state, q_part, key_piece, value_piece, key_rows):
        count = key_piece.shape[0]
        if count <= span:
            return attend_block(state, q_part, key_piece, value_piece, key_rows)
        blocks = count // span
        whole = blocks * span
        width = key_piece.shape[1]
        key_blocks = key_piece[:whole].reshape(blocks, span, width)
        value_blocks = value_piece[:whole].reshape(blocks, span, width)
        row_blocks = key_rows[:whole].reshape(blocks, span)

        def step_fn(carry, item):
            return (attend_block(carry, q_part, item[0], item[1], item[2]), None)

        state, _ = lax.scan(step_fn, state, (key_blocks, value_blocks, row_blocks))
        if whole < count:
            state = attend_block(state, q_part, key_piece[whole:], value_piece[whole:], key_rows[whole:])
        return state

    outer = lax.axis_size("c0")
    inner = lax.axis_size(INNER)
    rows_each = out_weight.shape[0]
    weight_rows = ring_pieces(out_weight, "c0")
    arrival = (lax.axis_index("c0") - jnp.arange(outer, dtype=jnp.int32)) % outer
    half = kv_local // 2
    splits = [(0, half, ("c0", "c2", "c1")), (half, kv_local, ("c0", "c1", "c2"))]
    gathered, bounds = [], []
    for first, last, order in splits:
        if last == first:
            continue
        cols = slice(first * HEAD_WIDTH, last * HEAD_WIDTH)
        for got, source in gather_order(jnp.concatenate([keys[:, cols], values[:, cols]], axis=1), order):
            key_rows = (source[:, None] * tok_dev + jnp.arange(tok_dev, dtype=jnp.int32)[None, :]).reshape(-1)
            gathered.append((got.reshape(key_rows.shape[0], -1), key_rows))
            bounds.append((first, last))
    gathered, weight_rows = lax.optimization_barrier((gathered, weight_rows))
    numerators, denominators = [], []
    states = {}
    for (first, last), (got, key_rows) in zip(bounds, gathered):
        width = (last - first) * HEAD_WIDTH
        q_part = q_groups[:, first:last]
        state = states.get((first, last), (
            jnp.zeros((last - first, group_repeat, tok_dev, HEAD_WIDTH), jnp.float32),
            jnp.zeros((last - first, group_repeat, tok_dev), jnp.float32),
        ))
        states[(first, last)] = attend(state, q_part, got[:, :width], got[:, width:], key_rows)
    for key in sorted(states):
        numerators.append(states[key][0])
        denominators.append(states[key][1])
    numerator = jnp.concatenate(numerators, axis=0)
    denominator = jnp.concatenate(denominators, axis=0)
    attended = (numerator / denominator[..., None]).astype(jnp.bfloat16)
    attended = attended.transpose(2, 0, 1, 3).reshape(tok_dev, kv_local * group_repeat * HEAD_WIDTH)
    all_heads = ring_all_gather(attended, "head").transpose(1, 0, 2).reshape(tok_dev, -1)
    blocks = all_heads.reshape(tok_dev, outer, inner, rows_each).transpose(2, 0, 1, 3)
    regrouped = permute_all_to_all(blocks, INNER)
    regrouped = jnp.take(regrouped.reshape(inner * tok_dev, outer, rows_each), arrival, axis=1)
    partial = jnp.dot(regrouped[:, 0], weight_rows[0], preferred_element_type=jnp.float32)
    for t in range(1, outer):
        partial = partial + jnp.dot(regrouped[:, t], weight_rows[t], preferred_element_type=jnp.float32)
    by_dest = partial.reshape(2, 2, tok_dev, -1)
    cut = by_dest.shape[-1] // 2
    mixed = jnp.concatenate([
        swap_reduce_scatter(by_dest[..., :cut], "c2", "c1"),
        swap_reduce_scatter(by_dest[..., cut:].transpose(1, 0, 2, 3), "c1", "c2"),
    ], axis=-1)
    hidden = hidden_in.astype(jnp.float32)
    sums = lax.psum(
        jnp.stack([
            jnp.sum(mixed * mixed, axis=1),
            jnp.sum(hidden * reward_weight[None, :], axis=1),
            jnp.sum(mixed * (out_gain * reward_weight)[None, :], axis=1),
        ]),
        "head",
    )
    rms = jnp.sqrt(sums[0] / D + 1e-06)
    normed = mixed / rms[:, None]
    out32 = hidden + normed * out_gain[None, :]
    tok_reward = sums[1] + sums[2] / rms
    onehot = (query_doc[:, None] == jnp.arange(NDOC, dtype=jnp.int32)[None, :]).astype(jnp.float32)
    partial_sums = jnp.sum(onehot * tok_reward[:, None], axis=0)
    totals = butterfly_sum(partial_sums, CTX)
    rewards = totals / jnp.sqrt(doc_lengths.astype(jnp.float32))
    return (out32.astype(jnp.bfloat16), rewards)


def solution(mesh):
    n_ctx, n_head = mesh.devices.shape
    split = Mesh(mesh.devices.reshape(n_ctx // 4, 2, 2, n_head), CTX + ("head",))
    rows = P(CTX, "head")
    in_specs = (rows, rows, rows, rows, rows, P("head"), P("head"), P())
    out_specs = (rows, P())
    return jax.shard_map(shards, mesh=split, in_specs=in_specs, out_specs=out_specs, check_vma=False)
```

```python
import jax
import jax.numpy as jnp
from jax import lax
from jax.sharding import Mesh, PartitionSpec as P

D = 4608
QUERY_HEADS = 32
KEY_VALUE_HEADS = 16
HEAD_WIDTH = 128
NDOC = 16


soft_cap = 50.0
CTX = ("c0", "c1", "c2")
INNER = ("c1", "c2")


def storage_positions(rows, tok_dev, n_ctx):
    owner = rows // tok_dev
    offset = rows % tok_dev
    half = tok_dev // 2
    slab = jnp.where(offset < half, owner, 2 * n_ctx - 1 - owner)
    return slab * half + offset % half


def document_of(positions, doc_ends):
    return jnp.sum((positions[:, None] >= doc_ends[None, :]).astype(jnp.int32), axis=1)


def ring_pieces(x, axis):
    n = lax.axis_size(axis)
    pieces = [x]
    for _ in range(n - 1):
        pieces.append(lax.ppermute(pieces[-1], axis, [(k, (k + 1) % n) for k in range(n)]))
    return pieces


def ring_gather(x, axis):
    return jnp.stack(ring_pieces(x, axis))


def gather_order(x, order):
    stride = {"c2": 1, "c1": lax.axis_size("c2"), "c0": lax.axis_size("c1") * lax.axis_size("c2")}
    source = jnp.zeros((), jnp.int32)
    for axis in order[:-1]:
        x = ring_gather(x, axis)
        n = lax.axis_size(axis)
        came = (lax.axis_index(axis) - jnp.arange(n, dtype=jnp.int32)) % n
        source = came.reshape((n,) + (1,) * source.ndim) * stride[axis] + source[None]
    last = order[-1]
    n = lax.axis_size(last)
    own = lax.axis_index(last)
    return [
        (piece, (((own - t) % n) * stride[last] + source).reshape(-1))
        for t, piece in enumerate(ring_pieces(x, last))
    ]


def ring_all_gather(x, axis):
    n = lax.axis_size(axis)
    arrived = ring_gather(x, axis)[::-1]
    return jnp.roll(arrived, lax.axis_index(axis) + 1, axis=0)


def permute_all_to_all(x, axes):
    n = lax.axis_size(axes)
    own = lax.axis_index(axes)
    pieces = [lax.dynamic_index_in_dim(x, own, axis=0, keepdims=False)]
    for shift in range(1, n):
        sent = lax.dynamic_index_in_dim(x, (own + shift) % n, axis=0, keepdims=False)
        pieces.append(lax.ppermute(sent, axes, [(k, (k + shift) % n) for k in range(n)]))
    return jnp.roll(jnp.stack(pieces[::-1]), own + 1, axis=0)


def permute_reduce_scatter(x, axes):
    n = lax.axis_size(axes)
    own = lax.axis_index(axes)
    total = lax.dynamic_index_in_dim(x, own, axis=0, keepdims=False)
    for shift in range(1, n):
        sent = lax.dynamic_index_in_dim(x, (own + shift) % n, axis=0, keepdims=False)
        total = total + lax.ppermute(sent, axes, [(k, (k + shift) % n) for k in range(n)])
    return total


def swap_reduce_scatter(x, first, second):
    own_first = lax.axis_index(first)
    own_second = lax.axis_index(second)
    keep = lax.dynamic_index_in_dim(x, own_first, axis=1, keepdims=False)
    sent = lax.dynamic_index_in_dim(x, 1 - own_first, axis=1, keepdims=False)
    keep = keep + lax.ppermute(sent, first, [(0, 1), (1, 0)])
    mine = lax.dynamic_index_in_dim(keep, own_second, axis=0, keepdims=False)
    sent = lax.dynamic_index_in_dim(keep, 1 - own_second, axis=0, keepdims=False)
    return mine + lax.ppermute(sent, second, [(0, 1), (1, 0)])


def butterfly_sum(x, axes):
    for axis in axes:
        size = lax.axis_size(axis)
        bit = 1
        while bit < size:
            x = x + lax.ppermute(x, axis, [(i, i ^ bit) for i in range(size)])
            bit *= 2
    return x


def shards(queries, keys, values, hidden_in, out_weight, out_gain, reward_weight, doc_lengths):
    n_ctx = lax.axis_size(CTX)
    device = lax.axis_index(CTX)
    tok_dev = queries.shape[0]
    kv_local = keys.shape[1] // HEAD_WIDTH
    group_repeat = QUERY_HEADS // KEY_VALUE_HEADS
    scale = (D / QUERY_HEADS) ** (-0.5)
    doc_ends = jnp.cumsum(doc_lengths)
    local_rows = device * tok_dev + jnp.arange(tok_dev, dtype=jnp.int32)
    query_pos = storage_positions(local_rows, tok_dev, n_ctx)
    query_doc = document_of(query_pos, doc_ends)
    q_groups = queries.reshape(tok_dev, kv_local, group_repeat, HEAD_WIDTH)
    span = tok_dev * max(1, 2048 // tok_dev)

    def attend_block(state, q_part, key_piece, value_piece, key_rows):
        count = key_piece.shape[0]
        heads = q_part.shape[1]
        key_pos = storage_positions(key_rows, tok_dev, n_ctx)
        key_doc = document_of(key_pos, doc_ends)
        visible = (query_doc[:, None] == key_doc[None, :]) & (
            key_pos[None, :] <= query_pos[:, None]
        )

        def compute(carry):
            numerator, denominator = carry
            scores = (
                jnp.einsum(
                    "qgrd,kgd->grqk",
                    q_part,
                    key_piece.reshape(count, heads, HEAD_WIDTH),
                    preferred_element_type=jnp.float32,
                )
                * scale
            )
            scores = soft_cap * jnp.tanh(scores / soft_cap)
            weights = jnp.where(visible[None, None], jnp.exp(scores), 0.0)
            numerator = numerator + jnp.einsum(
                "grqk,kgd->grqd",
                weights.astype(jnp.bfloat16),
                value_piece.reshape(count, heads, HEAD_WIDTH),
                preferred_element_type=jnp.float32,
            )
            denominator = denominator + jnp.sum(weights, axis=-1)
            return (numerator, denominator)

        if count <= span:
            return compute(state)
        return lax.cond(jnp.any(visible), compute, lambda carry: carry, state)

    def attend(state, q_part, key_piece, value_piece, key_rows):
        count = key_piece.shape[0]
        if count <= span:
            return attend_block(state, q_part, key_piece, value_piece, key_rows)
        blocks = count // span
        whole = blocks * span
        width = key_piece.shape[1]
        key_blocks = key_piece[:whole].reshape(blocks, span, width)
        value_blocks = value_piece[:whole].reshape(blocks, span, width)
        row_blocks = key_rows[:whole].reshape(blocks, span)

        def step_fn(carry, item):
            return (attend_block(carry, q_part, item[0], item[1], item[2]), None)

        state, _ = lax.scan(step_fn, state, (key_blocks, value_blocks, row_blocks))
        if whole < count:
            state = attend_block(state, q_part, key_piece[whole:], value_piece[whole:], key_rows[whole:])
        return state

    outer = lax.axis_size("c0")
    inner = lax.axis_size(INNER)
    rows_each = out_weight.shape[0]
    weight_rows = ring_pieces(out_weight, "c0")
    arrival = (lax.axis_index("c0") - jnp.arange(outer, dtype=jnp.int32)) % outer
    half = kv_local // 2
    splits = [(0, half, ("c0", "c2", "c1")), (half, kv_local, ("c0", "c1", "c2"))]
    gathered, bounds = [], []
    for first, last, order in splits:
        if last == first:
            continue
        cols = slice(first * HEAD_WIDTH, last * HEAD_WIDTH)
        for got, source in gather_order(jnp.concatenate([keys[:, cols], values[:, cols]], axis=1), order):
            key_rows = (source[:, None] * tok_dev + jnp.arange(tok_dev, dtype=jnp.int32)[None, :]).reshape(-1)
            gathered.append((got.reshape(key_rows.shape[0], -1), key_rows))
            bounds.append((first, last))
    late = [len(gathered) - 1 - k for k in range(len(gathered)) if k % 2 == 0]
    held, weight_rows = lax.optimization_barrier(([gathered[k] for k in late], weight_rows))
    for k, piece in zip(late, held):
        gathered[k] = piece
    numerators, denominators = [], []
    states = {}
    for (first, last), (got, key_rows) in zip(bounds, gathered):
        width = (last - first) * HEAD_WIDTH
        q_part = q_groups[:, first:last]
        state = states.get((first, last), (
            jnp.zeros((last - first, group_repeat, tok_dev, HEAD_WIDTH), jnp.float32),
            jnp.zeros((last - first, group_repeat, tok_dev), jnp.float32),
        ))
        states[(first, last)] = attend(state, q_part, got[:, :width], got[:, width:], key_rows)
    for key in sorted(states):
        numerators.append(states[key][0])
        denominators.append(states[key][1])
    numerator = jnp.concatenate(numerators, axis=0)
    denominator = jnp.concatenate(denominators, axis=0)
    attended = (numerator / denominator[..., None]).astype(jnp.bfloat16)
    attended = attended.transpose(2, 0, 1, 3).reshape(tok_dev, kv_local * group_repeat * HEAD_WIDTH)
    all_heads = ring_all_gather(attended, "head").transpose(1, 0, 2).reshape(tok_dev, -1)
    blocks = all_heads.reshape(tok_dev, outer, inner, rows_each).transpose(2, 0, 1, 3)
    regrouped = permute_all_to_all(blocks, INNER)
    regrouped = jnp.take(regrouped.reshape(inner * tok_dev, outer, rows_each), arrival, axis=1)
    partial = jnp.dot(regrouped[:, 0], weight_rows[0], preferred_element_type=jnp.float32)
    for t in range(1, outer):
        partial = partial + jnp.dot(regrouped[:, t], weight_rows[t], preferred_element_type=jnp.float32)
    by_dest = partial.reshape(2, 2, tok_dev, -1)
    cut = by_dest.shape[-1] // 2
    mixed = jnp.concatenate([
        swap_reduce_scatter(by_dest[..., :cut], "c2", "c1"),
        swap_reduce_scatter(by_dest[..., cut:].transpose(1, 0, 2, 3), "c1", "c2"),
    ], axis=-1)
    hidden = hidden_in.astype(jnp.float32)
    sums = lax.psum(
        jnp.stack([
            jnp.sum(mixed * mixed, axis=1),
            jnp.sum(hidden * reward_weight[None, :], axis=1),
            jnp.sum(mixed * (out_gain * reward_weight)[None, :], axis=1),
        ]),
        "head",
    )
    rms = jnp.sqrt(sums[0] / D + 1e-06)
    normed = mixed / rms[:, None]
    out32 = hidden + normed * out_gain[None, :]
    tok_reward = sums[1] + sums[2] / rms
    onehot = (query_doc[:, None] == jnp.arange(NDOC, dtype=jnp.int32)[None, :]).astype(jnp.float32)
    partial_sums = jnp.sum(onehot * tok_reward[:, None], axis=0)
    totals = butterfly_sum(partial_sums, CTX)
    rewards = totals / jnp.sqrt(doc_lengths.astype(jnp.float32))
    return (out32.astype(jnp.bfloat16), rewards)


def solution(mesh):
    n_ctx, n_head = mesh.devices.shape
    split = Mesh(mesh.devices.reshape(n_ctx // 4, 2, 2, n_head), CTX + ("head",))
    rows = P(CTX, "head")
    in_specs = (rows, rows, rows, rows, rows, P("head"), P("head"), P())
    out_specs = (rows, P())
    return jax.shard_map(shards, mesh=split, in_specs=in_specs, out_specs=out_specs, check_vma=False)
```

```python
import jax
import jax.numpy as jnp
from jax import lax
from jax.sharding import Mesh, PartitionSpec as P

D = 4608
QUERY_HEADS = 32
KEY_VALUE_HEADS = 16
HEAD_WIDTH = 128
NDOC = 16


soft_cap = 50.0
CTX = ("c0", "c1", "c2")
INNER = ("c1", "c2")


def storage_positions(rows, tok_dev, n_ctx):
    owner = rows // tok_dev
    offset = rows % tok_dev
    half = tok_dev // 2
    slab = jnp.where(offset < half, owner, 2 * n_ctx - 1 - owner)
    return slab * half + offset % half


def document_of(positions, doc_ends):
    return jnp.sum((positions[:, None] >= doc_ends[None, :]).astype(jnp.int32), axis=1)


def ring_pieces(x, axis):
    n = lax.axis_size(axis)
    pieces = [x]
    for _ in range(n - 1):
        pieces.append(lax.ppermute(pieces[-1], axis, [(k, (k + 1) % n) for k in range(n)]))
    return pieces


def ring_gather(x, axis):
    return jnp.stack(ring_pieces(x, axis))


def gather_order(x, order):
    stride = {"c2": 1, "c1": lax.axis_size("c2"), "c0": lax.axis_size("c1") * lax.axis_size("c2")}
    source = jnp.zeros((), jnp.int32)
    for axis in order[:-1]:
        x = ring_gather(x, axis)
        n = lax.axis_size(axis)
        came = (lax.axis_index(axis) - jnp.arange(n, dtype=jnp.int32)) % n
        source = came.reshape((n,) + (1,) * source.ndim) * stride[axis] + source[None]
    last = order[-1]
    n = lax.axis_size(last)
    own = lax.axis_index(last)
    flat = x.reshape(-1, x.shape[-1])
    return [
        (piece.T, (((own - t) % n) * stride[last] + source).reshape(-1))
        for t, piece in enumerate(ring_pieces(flat.T, last))
    ]


def ring_all_gather(x, axis):
    n = lax.axis_size(axis)
    arrived = ring_gather(x, axis)[::-1]
    return jnp.roll(arrived, lax.axis_index(axis) + 1, axis=0)


def permute_all_to_all(x, axes):
    n = lax.axis_size(axes)
    own = lax.axis_index(axes)
    pieces = [lax.dynamic_index_in_dim(x, own, axis=0, keepdims=False)]
    for shift in range(1, n):
        sent = lax.dynamic_index_in_dim(x, (own + shift) % n, axis=0, keepdims=False)
        pieces.append(lax.ppermute(sent, axes, [(k, (k + shift) % n) for k in range(n)]))
    return jnp.roll(jnp.stack(pieces[::-1]), own + 1, axis=0)


def permute_reduce_scatter(x, axes):
    n = lax.axis_size(axes)
    own = lax.axis_index(axes)
    total = lax.dynamic_index_in_dim(x, own, axis=0, keepdims=False)
    for shift in range(1, n):
        sent = lax.dynamic_index_in_dim(x, (own + shift) % n, axis=0, keepdims=False)
        total = total + lax.ppermute(sent, axes, [(k, (k + shift) % n) for k in range(n)])
    return total


def swap_reduce_scatter(x, first, second):
    own_first = lax.axis_index(first)
    own_second = lax.axis_index(second)
    keep = lax.dynamic_index_in_dim(x, own_first, axis=1, keepdims=False)
    sent = lax.dynamic_index_in_dim(x, 1 - own_first, axis=1, keepdims=False)
    keep = keep + lax.ppermute(sent, first, [(0, 1), (1, 0)])
    mine = lax.dynamic_index_in_dim(keep, own_second, axis=0, keepdims=False)
    sent = lax.dynamic_index_in_dim(keep, 1 - own_second, axis=0, keepdims=False)
    return mine + lax.ppermute(sent, second, [(0, 1), (1, 0)])


def butterfly_sum(x, axes):
    for axis in axes:
        size = lax.axis_size(axis)
        bit = 1
        while bit < size:
            x = x + lax.ppermute(x, axis, [(i, i ^ bit) for i in range(size)])
            bit *= 2
    return x


def shards(queries, keys, values, hidden_in, out_weight, out_gain, reward_weight, doc_lengths):
    n_ctx = lax.axis_size(CTX)
    device = lax.axis_index(CTX)
    tok_dev = queries.shape[0]
    kv_local = keys.shape[1] // HEAD_WIDTH
    group_repeat = QUERY_HEADS // KEY_VALUE_HEADS
    scale = (D / QUERY_HEADS) ** (-0.5)
    doc_ends = jnp.cumsum(doc_lengths)
    local_rows = device * tok_dev + jnp.arange(tok_dev, dtype=jnp.int32)
    query_pos = storage_positions(local_rows, tok_dev, n_ctx)
    query_doc = document_of(query_pos, doc_ends)
    q_groups = queries.reshape(tok_dev, kv_local, group_repeat, HEAD_WIDTH)
    span = tok_dev * max(1, 2048 // tok_dev)

    def attend_block(state, q_part, key_piece, value_piece, key_rows):
        count = key_piece.shape[0]
        heads = q_part.shape[1]
        key_pos = storage_positions(key_rows, tok_dev, n_ctx)
        key_doc = document_of(key_pos, doc_ends)
        visible = (query_doc[:, None] == key_doc[None, :]) & (
            key_pos[None, :] <= query_pos[:, None]
        )

        def compute(carry):
            numerator, denominator = carry
            scores = (
                jnp.einsum(
                    "qgrd,kgd->grqk",
                    q_part,
                    key_piece.reshape(count, heads, HEAD_WIDTH),
                    preferred_element_type=jnp.float32,
                )
                * scale
            )
            scores = soft_cap * jnp.tanh(scores / soft_cap)
            weights = jnp.where(visible[None, None], jnp.exp(scores), 0.0)
            numerator = numerator + jnp.einsum(
                "grqk,kgd->grqd",
                weights.astype(jnp.bfloat16),
                value_piece.reshape(count, heads, HEAD_WIDTH),
                preferred_element_type=jnp.float32,
            )
            denominator = denominator + jnp.sum(weights, axis=-1)
            return (numerator, denominator)

        if count <= span:
            return compute(state)
        return lax.cond(jnp.any(visible), compute, lambda carry: carry, state)

    def attend(state, q_part, key_piece, value_piece, key_rows):
        count = key_piece.shape[0]
        if count <= span:
            return attend_block(state, q_part, key_piece, value_piece, key_rows)
        blocks = count // span
        whole = blocks * span
        width = key_piece.shape[1]
        key_blocks = key_piece[:whole].reshape(blocks, span, width)
        value_blocks = value_piece[:whole].reshape(blocks, span, width)
        row_blocks = key_rows[:whole].reshape(blocks, span)

        def step_fn(carry, item):
            return (attend_block(carry, q_part, item[0], item[1], item[2]), None)

        state, _ = lax.scan(step_fn, state, (key_blocks, value_blocks, row_blocks))
        if whole < count:
            state = attend_block(state, q_part, key_piece[whole:], value_piece[whole:], key_rows[whole:])
        return state

    outer = lax.axis_size("c0")
    inner = lax.axis_size(INNER)
    rows_each = out_weight.shape[0]
    weight_rows = ring_pieces(out_weight, "c0")
    arrival = (lax.axis_index("c0") - jnp.arange(outer, dtype=jnp.int32)) % outer
    half = kv_local // 2
    splits = [(0, half, ("c0", "c2", "c1")), (half, kv_local, ("c0", "c1", "c2"))]
    gathered, bounds = [], []
    for first, last, order in splits:
        if last == first:
            continue
        cols = slice(first * HEAD_WIDTH, last * HEAD_WIDTH)
        for got, source in gather_order(jnp.concatenate([keys[:, cols], values[:, cols]], axis=1), order):
            key_rows = (source[:, None] * tok_dev + jnp.arange(tok_dev, dtype=jnp.int32)[None, :]).reshape(-1)
            gathered.append((got.reshape(key_rows.shape[0], -1), key_rows))
            bounds.append((first, last))
    late = [len(gathered) - 1 - k for k in range(len(gathered)) if k % 2 == 0]
    held, weight_rows = lax.optimization_barrier(([gathered[k] for k in late], weight_rows))
    for k, piece in zip(late, held):
        gathered[k] = piece
    numerators, denominators = [], []
    states = {}
    for (first, last), (got, key_rows) in zip(bounds, gathered):
        width = (last - first) * HEAD_WIDTH
        q_part = q_groups[:, first:last]
        state = states.get((first, last), (
            jnp.zeros((last - first, group_repeat, tok_dev, HEAD_WIDTH), jnp.float32),
            jnp.zeros((last - first, group_repeat, tok_dev), jnp.float32),
        ))
        states[(first, last)] = attend(state, q_part, got[:, :width], got[:, width:], key_rows)
    for key in sorted(states):
        numerators.append(states[key][0])
        denominators.append(states[key][1])
    numerator = jnp.concatenate(numerators, axis=0)
    denominator = jnp.concatenate(denominators, axis=0)
    attended = (numerator / denominator[..., None]).astype(jnp.bfloat16)
    attended = attended.transpose(2, 0, 1, 3).reshape(tok_dev, kv_local * group_repeat * HEAD_WIDTH)
    all_heads = ring_all_gather(attended, "head").transpose(1, 0, 2).reshape(tok_dev, -1)
    blocks = all_heads.reshape(tok_dev, outer, inner, rows_each).transpose(2, 0, 1, 3)
    regrouped = permute_all_to_all(blocks, INNER)
    regrouped = jnp.take(regrouped.reshape(inner * tok_dev, outer, rows_each), arrival, axis=1)
    partial = jnp.dot(regrouped[:, 0], weight_rows[0], preferred_element_type=jnp.float32)
    for t in range(1, outer):
        partial = partial + jnp.dot(regrouped[:, t], weight_rows[t], preferred_element_type=jnp.float32)
    by_dest = partial.reshape(2, 2, tok_dev, -1)
    cut = by_dest.shape[-1] // 2
    mixed = jnp.concatenate([
        swap_reduce_scatter(by_dest[..., :cut], "c2", "c1"),
        swap_reduce_scatter(by_dest[..., cut:].transpose(1, 0, 2, 3), "c1", "c2"),
    ], axis=-1)
    hidden = hidden_in.astype(jnp.float32)
    sums = lax.psum(
        jnp.stack([
            jnp.sum(mixed * mixed, axis=1),
            jnp.sum(hidden * reward_weight[None, :], axis=1),
            jnp.sum(mixed * (out_gain * reward_weight)[None, :], axis=1),
        ]),
        "head",
    )
    rms = jnp.sqrt(sums[0] / D + 1e-06)
    normed = mixed / rms[:, None]
    out32 = hidden + normed * out_gain[None, :]
    tok_reward = sums[1] + sums[2] / rms
    onehot = (query_doc[:, None] == jnp.arange(NDOC, dtype=jnp.int32)[None, :]).astype(jnp.float32)
    partial_sums = jnp.sum(onehot * tok_reward[:, None], axis=0)
    totals = butterfly_sum(partial_sums, CTX)
    rewards = totals / jnp.sqrt(doc_lengths.astype(jnp.float32))
    return (out32.astype(jnp.bfloat16), rewards)


def solution(mesh):
    n_ctx, n_head = mesh.devices.shape
    split = Mesh(mesh.devices.reshape(n_ctx // 4, 2, 2, n_head), CTX + ("head",))
    rows = P(CTX, "head")
    in_specs = (rows, rows, rows, rows, rows, P("head"), P("head"), P())
    out_specs = (rows, P())
    return jax.shard_map(shards, mesh=split, in_specs=in_specs, out_specs=out_specs, check_vma=False)
```

```python
import jax
import jax.numpy as jnp
from jax import lax
from jax.sharding import Mesh, PartitionSpec as P

D = 4608
QUERY_HEADS = 32
KEY_VALUE_HEADS = 16
HEAD_WIDTH = 128
NDOC = 16


soft_cap = 50.0
CTX = ("c0", "c1", "c2")
INNER = ("c1", "c2")


def storage_positions(rows, tok_dev, n_ctx):
    owner = rows // tok_dev
    offset = rows % tok_dev
    half = tok_dev // 2
    slab = jnp.where(offset < half, owner, 2 * n_ctx - 1 - owner)
    return slab * half + offset % half


def document_of(positions, doc_ends):
    return jnp.sum((positions[:, None] >= doc_ends[None, :]).astype(jnp.int32), axis=1)


def ring_pieces(x, axis):
    n = lax.axis_size(axis)
    pieces = [x]
    for _ in range(n - 1):
        pieces.append(lax.ppermute(pieces[-1], axis, [(k, (k + 1) % n) for k in range(n)]))
    return pieces


def ring_gather(x, axis):
    return jnp.stack(ring_pieces(x, axis))


def gather_order(x, order):
    stride = {"c2": 1, "c1": lax.axis_size("c2"), "c0": lax.axis_size("c1") * lax.axis_size("c2")}
    source = jnp.zeros((), jnp.int32)
    x = x.T
    for axis in order[:-1]:
        x = jnp.concatenate(ring_pieces(x, axis), axis=1)
        n = lax.axis_size(axis)
        came = (lax.axis_index(axis) - jnp.arange(n, dtype=jnp.int32)) % n
        source = came.reshape((n,) + (1,) * source.ndim) * stride[axis] + source[None]
    last = order[-1]
    n = lax.axis_size(last)
    own = lax.axis_index(last)
    return [
        (piece.T, (((own - t) % n) * stride[last] + source).reshape(-1))
        for t, piece in enumerate(ring_pieces(x, last))
    ]


def ring_all_gather(x, axis):
    n = lax.axis_size(axis)
    arrived = ring_gather(x, axis)[::-1]
    return jnp.roll(arrived, lax.axis_index(axis) + 1, axis=0)


def permute_all_to_all(x, axes):
    n = lax.axis_size(axes)
    own = lax.axis_index(axes)
    pieces = [lax.dynamic_index_in_dim(x, own, axis=0, keepdims=False)]
    for shift in range(1, n):
        sent = lax.dynamic_index_in_dim(x, (own + shift) % n, axis=0, keepdims=False)
        pieces.append(lax.ppermute(sent, axes, [(k, (k + shift) % n) for k in range(n)]))
    return jnp.roll(jnp.stack(pieces[::-1]), own + 1, axis=0)


def permute_reduce_scatter(x, axes):
    n = lax.axis_size(axes)
    own = lax.axis_index(axes)
    total = lax.dynamic_index_in_dim(x, own, axis=0, keepdims=False)
    for shift in range(1, n):
        sent = lax.dynamic_index_in_dim(x, (own + shift) % n, axis=0, keepdims=False)
        total = total + lax.ppermute(sent, axes, [(k, (k + shift) % n) for k in range(n)])
    return total


def swap_reduce_scatter(x, first, second):
    own_first = lax.axis_index(first)
    own_second = lax.axis_index(second)
    keep = lax.dynamic_index_in_dim(x, own_first, axis=1, keepdims=False)
    sent = lax.dynamic_index_in_dim(x, 1 - own_first, axis=1, keepdims=False)
    keep = keep + lax.ppermute(sent, first, [(0, 1), (1, 0)])
    mine = lax.dynamic_index_in_dim(keep, own_second, axis=0, keepdims=False)
    sent = lax.dynamic_index_in_dim(keep, 1 - own_second, axis=0, keepdims=False)
    return mine + lax.ppermute(sent, second, [(0, 1), (1, 0)])


def butterfly_sum(x, axes):
    for axis in axes:
        size = lax.axis_size(axis)
        bit = 1
        while bit < size:
            x = x + lax.ppermute(x, axis, [(i, i ^ bit) for i in range(size)])
            bit *= 2
    return x


def shards(queries, keys, values, hidden_in, out_weight, out_gain, reward_weight, doc_lengths):
    n_ctx = lax.axis_size(CTX)
    device = lax.axis_index(CTX)
    tok_dev = queries.shape[0]
    kv_local = keys.shape[1] // HEAD_WIDTH
    group_repeat = QUERY_HEADS // KEY_VALUE_HEADS
    scale = (D / QUERY_HEADS) ** (-0.5)
    doc_ends = jnp.cumsum(doc_lengths)
    local_rows = device * tok_dev + jnp.arange(tok_dev, dtype=jnp.int32)
    query_pos = storage_positions(local_rows, tok_dev, n_ctx)
    query_doc = document_of(query_pos, doc_ends)
    q_groups = queries.reshape(tok_dev, kv_local, group_repeat, HEAD_WIDTH)
    span = tok_dev * max(1, 2048 // tok_dev)

    def attend_block(state, q_part, key_piece, value_piece, key_rows):
        count = key_piece.shape[0]
        heads = q_part.shape[1]
        key_pos = storage_positions(key_rows, tok_dev, n_ctx)
        key_doc = document_of(key_pos, doc_ends)
        visible = (query_doc[:, None] == key_doc[None, :]) & (
            key_pos[None, :] <= query_pos[:, None]
        )

        def compute(carry):
            numerator, denominator = carry
            scores = (
                jnp.einsum(
                    "qgrd,kgd->grqk",
                    q_part,
                    key_piece.reshape(count, heads, HEAD_WIDTH),
                    preferred_element_type=jnp.float32,
                )
                * scale
            )
            scores = soft_cap * jnp.tanh(scores / soft_cap)
            weights = jnp.where(visible[None, None], jnp.exp(scores), 0.0)
            numerator = numerator + jnp.einsum(
                "grqk,kgd->grqd",
                weights.astype(jnp.bfloat16),
                value_piece.reshape(count, heads, HEAD_WIDTH),
                preferred_element_type=jnp.float32,
            )
            denominator = denominator + jnp.sum(weights, axis=-1)
            return (numerator, denominator)

        if count <= span:
            return compute(state)
        return lax.cond(jnp.any(visible), compute, lambda carry: carry, state)

    def attend(state, q_part, key_piece, value_piece, key_rows):
        count = key_piece.shape[0]
        if count <= span:
            return attend_block(state, q_part, key_piece, value_piece, key_rows)
        blocks = count // span
        whole = blocks * span
        width = key_piece.shape[1]
        key_blocks = key_piece[:whole].reshape(blocks, span, width)
        value_blocks = value_piece[:whole].reshape(blocks, span, width)
        row_blocks = key_rows[:whole].reshape(blocks, span)

        def step_fn(carry, item):
            return (attend_block(carry, q_part, item[0], item[1], item[2]), None)

        state, _ = lax.scan(step_fn, state, (key_blocks, value_blocks, row_blocks))
        if whole < count:
            state = attend_block(state, q_part, key_piece[whole:], value_piece[whole:], key_rows[whole:])
        return state

    outer = lax.axis_size("c0")
    inner = lax.axis_size(INNER)
    rows_each = out_weight.shape[0]
    weight_rows = ring_pieces(out_weight, "c0")
    arrival = (lax.axis_index("c0") - jnp.arange(outer, dtype=jnp.int32)) % outer
    half = kv_local // 2
    splits = [(0, half, ("c0", "c2", "c1")), (half, kv_local, ("c0", "c1", "c2"))]
    gathered, bounds = [], []
    for first, last, order in splits:
        if last == first:
            continue
        cols = slice(first * HEAD_WIDTH, last * HEAD_WIDTH)
        for got, source in gather_order(jnp.concatenate([keys[:, cols], values[:, cols]], axis=1), order):
            key_rows = (source[:, None] * tok_dev + jnp.arange(tok_dev, dtype=jnp.int32)[None, :]).reshape(-1)
            gathered.append((got.reshape(key_rows.shape[0], -1), key_rows))
            bounds.append((first, last))
    late = [len(gathered) - 1 - k for k in range(len(gathered)) if k % 2 == 0]
    held, weight_rows = lax.optimization_barrier(([gathered[k] for k in late], weight_rows))
    for k, piece in zip(late, held):
        gathered[k] = piece
    numerators, denominators = [], []
    states = {}
    for (first, last), (got, key_rows) in zip(bounds, gathered):
        width = (last - first) * HEAD_WIDTH
        q_part = q_groups[:, first:last]
        state = states.get((first, last), (
            jnp.zeros((last - first, group_repeat, tok_dev, HEAD_WIDTH), jnp.float32),
            jnp.zeros((last - first, group_repeat, tok_dev), jnp.float32),
        ))
        states[(first, last)] = attend(state, q_part, got[:, :width], got[:, width:], key_rows)
    for key in sorted(states):
        numerators.append(states[key][0])
        denominators.append(states[key][1])
    numerator = jnp.concatenate(numerators, axis=0)
    denominator = jnp.concatenate(denominators, axis=0)
    attended = (numerator / denominator[..., None]).astype(jnp.bfloat16)
    attended = attended.transpose(2, 0, 1, 3).reshape(tok_dev, kv_local * group_repeat * HEAD_WIDTH)
    all_heads = ring_all_gather(attended, "head").transpose(1, 0, 2).reshape(tok_dev, -1)
    blocks = all_heads.reshape(tok_dev, outer, inner, rows_each).transpose(2, 0, 1, 3)
    regrouped = permute_all_to_all(blocks, INNER)
    regrouped = jnp.take(regrouped.reshape(inner * tok_dev, outer, rows_each), arrival, axis=1)
    partial = jnp.dot(regrouped[:, 0], weight_rows[0], preferred_element_type=jnp.float32)
    for t in range(1, outer):
        partial = partial + jnp.dot(regrouped[:, t], weight_rows[t], preferred_element_type=jnp.float32)
    by_dest = partial.reshape(2, 2, tok_dev, -1)
    cut = by_dest.shape[-1] // 2
    mixed = jnp.concatenate([
        swap_reduce_scatter(by_dest[..., :cut], "c2", "c1"),
        swap_reduce_scatter(by_dest[..., cut:].transpose(1, 0, 2, 3), "c1", "c2"),
    ], axis=-1)
    hidden = hidden_in.astype(jnp.float32)
    sums = lax.psum(
        jnp.stack([
            jnp.sum(mixed * mixed, axis=1),
            jnp.sum(hidden * reward_weight[None, :], axis=1),
            jnp.sum(mixed * (out_gain * reward_weight)[None, :], axis=1),
        ]),
        "head",
    )
    rms = jnp.sqrt(sums[0] / D + 1e-06)
    normed = mixed / rms[:, None]
    out32 = hidden + normed * out_gain[None, :]
    tok_reward = sums[1] + sums[2] / rms
    onehot = (query_doc[:, None] == jnp.arange(NDOC, dtype=jnp.int32)[None, :]).astype(jnp.float32)
    partial_sums = jnp.sum(onehot * tok_reward[:, None], axis=0)
    totals = butterfly_sum(partial_sums, CTX)
    rewards = totals / jnp.sqrt(doc_lengths.astype(jnp.float32))
    return (out32.astype(jnp.bfloat16), rewards)


def solution(mesh):
    n_ctx, n_head = mesh.devices.shape
    split = Mesh(mesh.devices.reshape(n_ctx // 4, 2, 2, n_head), CTX + ("head",))
    rows = P(CTX, "head")
    in_specs = (rows, rows, rows, rows, rows, P("head"), P("head"), P())
    out_specs = (rows, P())
    return jax.shard_map(shards, mesh=split, in_specs=in_specs, out_specs=out_specs, check_vma=False)
```

```python
import jax
import jax.numpy as jnp
from jax import lax
from jax.sharding import Mesh, PartitionSpec as P

D = 4608
QUERY_HEADS = 32
KEY_VALUE_HEADS = 16
HEAD_WIDTH = 128
NDOC = 16


soft_cap = 50.0
CTX = ("c0", "c1", "c2")
INNER = ("c1", "c2")


def storage_positions(rows, tok_dev, n_ctx):
    owner = rows // tok_dev
    offset = rows % tok_dev
    half = tok_dev // 2
    slab = jnp.where(offset < half, owner, 2 * n_ctx - 1 - owner)
    return slab * half + offset % half


def document_of(positions, doc_ends):
    return jnp.sum((positions[:, None] >= doc_ends[None, :]).astype(jnp.int32), axis=1)


def ring_pieces(x, axis):
    n = lax.axis_size(axis)
    pieces = [x]
    for _ in range(n - 1):
        pieces.append(lax.ppermute(pieces[-1], axis, [(k, (k + 1) % n) for k in range(n)]))
    return pieces


def ring_gather(x, axis):
    return jnp.stack(ring_pieces(x, axis))


def gather_order(x, order):
    stride = {"c2": 1, "c1": lax.axis_size("c2"), "c0": lax.axis_size("c1") * lax.axis_size("c2")}
    source = jnp.zeros((), jnp.int32)
    for axis in order[:-1]:
        x = ring_gather(x, axis)
        n = lax.axis_size(axis)
        came = (lax.axis_index(axis) - jnp.arange(n, dtype=jnp.int32)) % n
        source = came.reshape((n,) + (1,) * source.ndim) * stride[axis] + source[None]
    last = order[-1]
    n = lax.axis_size(last)
    own = lax.axis_index(last)
    return [
        (piece, (((own - t) % n) * stride[last] + source).reshape(-1))
        for t, piece in enumerate(ring_pieces(x, last))
    ]


def ring_all_gather(x, axis):
    n = lax.axis_size(axis)
    arrived = ring_gather(x, axis)[::-1]
    return jnp.roll(arrived, lax.axis_index(axis) + 1, axis=0)


def permute_all_to_all(x, axes):
    n = lax.axis_size(axes)
    own = lax.axis_index(axes)
    pieces = [lax.dynamic_index_in_dim(x, own, axis=0, keepdims=False)]
    for shift in range(1, n):
        sent = lax.dynamic_index_in_dim(x, (own + shift) % n, axis=0, keepdims=False)
        pieces.append(lax.ppermute(sent, axes, [(k, (k + shift) % n) for k in range(n)]))
    return jnp.roll(jnp.stack(pieces[::-1]), own + 1, axis=0)


def permute_reduce_scatter(x, axes):
    n = lax.axis_size(axes)
    own = lax.axis_index(axes)
    total = lax.dynamic_index_in_dim(x, own, axis=0, keepdims=False)
    for shift in range(1, n):
        sent = lax.dynamic_index_in_dim(x, (own + shift) % n, axis=0, keepdims=False)
        total = total + lax.ppermute(sent, axes, [(k, (k + shift) % n) for k in range(n)])
    return total


def swap_reduce_scatter(x, first, second):
    own_first = lax.axis_index(first)
    own_second = lax.axis_index(second)
    keep = lax.dynamic_index_in_dim(x, own_first, axis=1, keepdims=False)
    sent = lax.dynamic_index_in_dim(x, 1 - own_first, axis=1, keepdims=False)
    keep = keep + lax.ppermute(sent, first, [(0, 1), (1, 0)])
    mine = lax.dynamic_index_in_dim(keep, own_second, axis=0, keepdims=False)
    sent = lax.dynamic_index_in_dim(keep, 1 - own_second, axis=0, keepdims=False)
    return mine + lax.ppermute(sent, second, [(0, 1), (1, 0)])


def butterfly_sum(x, axes):
    for axis in axes:
        size = lax.axis_size(axis)
        bit = 1
        while bit < size:
            x = x + lax.ppermute(x, axis, [(i, i ^ bit) for i in range(size)])
            bit *= 2
    return x


def shards(queries, keys, values, hidden_in, out_weight, out_gain, reward_weight, doc_lengths):
    n_ctx = lax.axis_size(CTX)
    device = lax.axis_index(CTX)
    tok_dev = queries.shape[0]
    kv_local = keys.shape[1] // HEAD_WIDTH
    group_repeat = QUERY_HEADS // KEY_VALUE_HEADS
    scale = (D / QUERY_HEADS) ** (-0.5)
    doc_ends = jnp.cumsum(doc_lengths)
    local_rows = device * tok_dev + jnp.arange(tok_dev, dtype=jnp.int32)
    query_pos = storage_positions(local_rows, tok_dev, n_ctx)
    query_doc = document_of(query_pos, doc_ends)
    q_groups = queries.reshape(tok_dev, kv_local, group_repeat, HEAD_WIDTH)
    span = tok_dev * max(1, 2048 // tok_dev)

    def attend_block(state, q_part, key_piece, value_piece, key_rows):
        count = key_piece.shape[0]
        heads = q_part.shape[1]
        key_pos = storage_positions(key_rows, tok_dev, n_ctx)
        key_doc = document_of(key_pos, doc_ends)
        visible = (query_doc[:, None] == key_doc[None, :]) & (
            key_pos[None, :] <= query_pos[:, None]
        )

        def compute(carry):
            numerator, denominator = carry
            scores = (
                jnp.einsum(
                    "qgrd,kgd->grqk",
                    q_part,
                    key_piece.reshape(count, heads, HEAD_WIDTH),
                    preferred_element_type=jnp.float32,
                )
                * scale
            )
            scores = soft_cap * jnp.tanh(scores / soft_cap)
            weights = jnp.where(visible[None, None], jnp.exp(scores), 0.0)
            numerator = numerator + jnp.einsum(
                "grqk,kgd->grqd",
                weights.astype(jnp.bfloat16),
                value_piece.reshape(count, heads, HEAD_WIDTH),
                preferred_element_type=jnp.float32,
            )
            denominator = denominator + jnp.sum(weights, axis=-1)
            return (numerator, denominator)

        if count <= span:
            return compute(state)
        return lax.cond(jnp.any(visible), compute, lambda carry: carry, state)

    def attend(state, q_part, key_piece, value_piece, key_rows):
        count = key_piece.shape[0]
        if count <= span:
            return attend_block(state, q_part, key_piece, value_piece, key_rows)
        blocks = count // span
        whole = blocks * span
        width = key_piece.shape[1]
        key_blocks = key_piece[:whole].reshape(blocks, span, width)
        value_blocks = value_piece[:whole].reshape(blocks, span, width)
        row_blocks = key_rows[:whole].reshape(blocks, span)

        def step_fn(carry, item):
            return (attend_block(carry, q_part, item[0], item[1], item[2]), None)

        state, _ = lax.scan(step_fn, state, (key_blocks, value_blocks, row_blocks))
        if whole < count:
            state = attend_block(state, q_part, key_piece[whole:], value_piece[whole:], key_rows[whole:])
        return state

    outer = lax.axis_size("c0")
    inner = lax.axis_size(INNER)
    rows_each = out_weight.shape[0]
    weight_rows = ring_pieces(out_weight, "c0")
    arrival = (lax.axis_index("c0") - jnp.arange(outer, dtype=jnp.int32)) % outer
    half = kv_local // 2
    splits = [(0, half, ("c0", "c2", "c1")), (half, kv_local, ("c0", "c1", "c2"))]
    gathered, bounds = [], []
    for first, last, order in splits:
        if last == first:
            continue
        cols = slice(first * HEAD_WIDTH, last * HEAD_WIDTH)
        for got, source in gather_order(jnp.concatenate([keys[:, cols], values[:, cols]], axis=1), order):
            key_rows = (source[:, None] * tok_dev + jnp.arange(tok_dev, dtype=jnp.int32)[None, :]).reshape(-1)
            gathered.append((got.reshape(key_rows.shape[0], -1), key_rows))
            bounds.append((first, last))
    late = [len(gathered) - 1 - k for k in range(len(gathered)) if k % 2 == 0]
    held, weight_rows = lax.optimization_barrier(([gathered[k] for k in late], weight_rows))
    for k, piece in zip(late, held):
        gathered[k] = piece
    numerators, denominators = [], []
    states = {}
    for (first, last), (got, key_rows) in zip(bounds, gathered):
        width = (last - first) * HEAD_WIDTH
        q_part = q_groups[:, first:last]
        state = states.get((first, last), (
            jnp.zeros((last - first, group_repeat, tok_dev, HEAD_WIDTH), jnp.float32),
            jnp.zeros((last - first, group_repeat, tok_dev), jnp.float32),
        ))
        states[(first, last)] = attend(state, q_part, got[:, :width], got[:, width:], key_rows)
    for key in sorted(states):
        numerators.append(states[key][0])
        denominators.append(states[key][1])
    numerator = jnp.concatenate(numerators, axis=0)
    denominator = jnp.concatenate(denominators, axis=0)
    attended = (numerator / denominator[..., None]).astype(jnp.bfloat16)
    attended = attended.transpose(2, 0, 1, 3).reshape(tok_dev, kv_local * group_repeat * HEAD_WIDTH)
    all_heads = ring_all_gather(attended, "head").transpose(1, 0, 2).reshape(tok_dev, -1)
    blocks = all_heads.reshape(tok_dev, outer, inner, rows_each).transpose(2, 0, 1, 3)
    regrouped = permute_all_to_all(blocks, INNER)
    regrouped = jnp.take(regrouped.reshape(inner * tok_dev, outer, rows_each), arrival, axis=1)
    cut = out_weight.shape[1] // 2

    def product(cols):
        total = jnp.dot(regrouped[:, 0], weight_rows[0][:, cols], preferred_element_type=jnp.float32)
        for t in range(1, outer):
            total = total + jnp.dot(regrouped[:, t], weight_rows[t][:, cols], preferred_element_type=jnp.float32)
        return total.reshape(2, 2, tok_dev, -1)

    first_half = swap_reduce_scatter(product(slice(0, cut)), "c2", "c1")
    second_half = swap_reduce_scatter(product(slice(cut, None)).transpose(1, 0, 2, 3), "c1", "c2")
    mixed = jnp.concatenate([first_half, second_half], axis=-1)
    hidden = hidden_in.astype(jnp.float32)
    sums = lax.psum(
        jnp.stack([
            jnp.sum(mixed * mixed, axis=1),
            jnp.sum(hidden * reward_weight[None, :], axis=1),
            jnp.sum(mixed * (out_gain * reward_weight)[None, :], axis=1),
        ]),
        "head",
    )
    rms = jnp.sqrt(sums[0] / D + 1e-06)
    normed = mixed / rms[:, None]
    out32 = hidden + normed * out_gain[None, :]
    tok_reward = sums[1] + sums[2] / rms
    onehot = (query_doc[:, None] == jnp.arange(NDOC, dtype=jnp.int32)[None, :]).astype(jnp.float32)
    partial_sums = jnp.sum(onehot * tok_reward[:, None], axis=0)
    totals = butterfly_sum(partial_sums, CTX)
    rewards = totals / jnp.sqrt(doc_lengths.astype(jnp.float32))
    return (out32.astype(jnp.bfloat16), rewards)


def solution(mesh):
    n_ctx, n_head = mesh.devices.shape
    split = Mesh(mesh.devices.reshape(n_ctx // 4, 2, 2, n_head), CTX + ("head",))
    rows = P(CTX, "head")
    in_specs = (rows, rows, rows, rows, rows, P("head"), P("head"), P())
    out_specs = (rows, P())
    return jax.shard_map(shards, mesh=split, in_specs=in_specs, out_specs=out_specs, check_vma=False)
```

```python
import jax
import jax.numpy as jnp
from jax import lax
from jax.sharding import Mesh, PartitionSpec as P

D = 4608
QUERY_HEADS = 32
KEY_VALUE_HEADS = 16
HEAD_WIDTH = 128
NDOC = 16


soft_cap = 50.0
CTX = ("c0", "c1", "c2")
INNER = ("c1", "c2")


def storage_positions(rows, tok_dev, n_ctx):
    owner = rows // tok_dev
    offset = rows % tok_dev
    half = tok_dev // 2
    slab = jnp.where(offset < half, owner, 2 * n_ctx - 1 - owner)
    return slab * half + offset % half


def document_of(positions, doc_ends):
    return jnp.sum((positions[:, None] >= doc_ends[None, :]).astype(jnp.int32), axis=1)


def ring_pieces(x, axis, direct=False):
    n = lax.axis_size(axis)
    pieces = [x]
    for t in range(1, n):
        if direct:
            pieces.append(lax.ppermute(x, axis, [(k, (k + t) % n) for k in range(n)]))
        else:
            pieces.append(lax.ppermute(pieces[-1], axis, [(k, (k + 1) % n) for k in range(n)]))
    return pieces


def ring_gather(x, axis):
    return jnp.stack(ring_pieces(x, axis))


def gather_order(x, order):
    stride = {"c2": 1, "c1": lax.axis_size("c2"), "c0": lax.axis_size("c1") * lax.axis_size("c2")}
    source = jnp.zeros((), jnp.int32)
    for stage, axis in enumerate(order[:-1]):
        x = jnp.stack(ring_pieces(x, axis, direct=stage == 0))
        n = lax.axis_size(axis)
        came = (lax.axis_index(axis) - jnp.arange(n, dtype=jnp.int32)) % n
        source = came.reshape((n,) + (1,) * source.ndim) * stride[axis] + source[None]
    last = order[-1]
    n = lax.axis_size(last)
    own = lax.axis_index(last)
    return [
        (piece, (((own - t) % n) * stride[last] + source).reshape(-1))
        for t, piece in enumerate(ring_pieces(x, last))
    ]


def ring_all_gather(x, axis):
    n = lax.axis_size(axis)
    arrived = ring_gather(x, axis)[::-1]
    return jnp.roll(arrived, lax.axis_index(axis) + 1, axis=0)


def permute_all_to_all(x, axes):
    n = lax.axis_size(axes)
    own = lax.axis_index(axes)
    pieces = [lax.dynamic_index_in_dim(x, own, axis=0, keepdims=False)]
    for shift in range(1, n):
        sent = lax.dynamic_index_in_dim(x, (own + shift) % n, axis=0, keepdims=False)
        pieces.append(lax.ppermute(sent, axes, [(k, (k + shift) % n) for k in range(n)]))
    return jnp.roll(jnp.stack(pieces[::-1]), own + 1, axis=0)


def permute_reduce_scatter(x, axes):
    n = lax.axis_size(axes)
    own = lax.axis_index(axes)
    total = lax.dynamic_index_in_dim(x, own, axis=0, keepdims=False)
    for shift in range(1, n):
        sent = lax.dynamic_index_in_dim(x, (own + shift) % n, axis=0, keepdims=False)
        total = total + lax.ppermute(sent, axes, [(k, (k + shift) % n) for k in range(n)])
    return total


def swap_reduce_scatter(x, first, second):
    own_first = lax.axis_index(first)
    own_second = lax.axis_index(second)
    keep = lax.dynamic_index_in_dim(x, own_first, axis=1, keepdims=False)
    sent = lax.dynamic_index_in_dim(x, 1 - own_first, axis=1, keepdims=False)
    keep = keep + lax.ppermute(sent, first, [(0, 1), (1, 0)])
    mine = lax.dynamic_index_in_dim(keep, own_second, axis=0, keepdims=False)
    sent = lax.dynamic_index_in_dim(keep, 1 - own_second, axis=0, keepdims=False)
    return mine + lax.ppermute(sent, second, [(0, 1), (1, 0)])


def butterfly_sum(x, axes):
    for axis in axes:
        size = lax.axis_size(axis)
        bit = 1
        while bit < size:
            x = x + lax.ppermute(x, axis, [(i, i ^ bit) for i in range(size)])
            bit *= 2
    return x


def shards(queries, keys, values, hidden_in, out_weight, out_gain, reward_weight, doc_lengths):
    n_ctx = lax.axis_size(CTX)
    device = lax.axis_index(CTX)
    tok_dev = queries.shape[0]
    kv_local = keys.shape[1] // HEAD_WIDTH
    group_repeat = QUERY_HEADS // KEY_VALUE_HEADS
    scale = (D / QUERY_HEADS) ** (-0.5)
    doc_ends = jnp.cumsum(doc_lengths)
    local_rows = device * tok_dev + jnp.arange(tok_dev, dtype=jnp.int32)
    query_pos = storage_positions(local_rows, tok_dev, n_ctx)
    query_doc = document_of(query_pos, doc_ends)
    q_groups = queries.reshape(tok_dev, kv_local, group_repeat, HEAD_WIDTH)
    span = tok_dev * max(1, 2048 // tok_dev)

    def attend_block(state, q_part, key_piece, value_piece, key_rows):
        count = key_piece.shape[0]
        heads = q_part.shape[1]
        key_pos = storage_positions(key_rows, tok_dev, n_ctx)
        key_doc = document_of(key_pos, doc_ends)
        visible = (query_doc[:, None] == key_doc[None, :]) & (
            key_pos[None, :] <= query_pos[:, None]
        )

        def compute(carry):
            numerator, denominator = carry
            scores = (
                jnp.einsum(
                    "qgrd,kgd->grqk",
                    q_part,
                    key_piece.reshape(count, heads, HEAD_WIDTH),
                    preferred_element_type=jnp.float32,
                )
                * scale
            )
            scores = soft_cap * jnp.tanh(scores / soft_cap)
            weights = jnp.where(visible[None, None], jnp.exp(scores), 0.0)
            numerator = numerator + jnp.einsum(
                "grqk,kgd->grqd",
                weights.astype(jnp.bfloat16),
                value_piece.reshape(count, heads, HEAD_WIDTH),
                preferred_element_type=jnp.float32,
            )
            denominator = denominator + jnp.sum(weights, axis=-1)
            return (numerator, denominator)

        if count <= span:
            return compute(state)
        return lax.cond(jnp.any(visible), compute, lambda carry: carry, state)

    def attend(state, q_part, key_piece, value_piece, key_rows):
        count = key_piece.shape[0]
        if count <= span:
            return attend_block(state, q_part, key_piece, value_piece, key_rows)
        blocks = count // span
        whole = blocks * span
        width = key_piece.shape[1]
        key_blocks = key_piece[:whole].reshape(blocks, span, width)
        value_blocks = value_piece[:whole].reshape(blocks, span, width)
        row_blocks = key_rows[:whole].reshape(blocks, span)

        def step_fn(carry, item):
            return (attend_block(carry, q_part, item[0], item[1], item[2]), None)

        state, _ = lax.scan(step_fn, state, (key_blocks, value_blocks, row_blocks))
        if whole < count:
            state = attend_block(state, q_part, key_piece[whole:], value_piece[whole:], key_rows[whole:])
        return state

    outer = lax.axis_size("c0")
    inner = lax.axis_size(INNER)
    rows_each = out_weight.shape[0]
    weight_rows = ring_pieces(out_weight, "c0")
    arrival = (lax.axis_index("c0") - jnp.arange(outer, dtype=jnp.int32)) % outer
    half = kv_local // 2
    splits = [(0, half, ("c0", "c2", "c1")), (half, kv_local, ("c0", "c1", "c2"))]
    gathered, bounds = [], []
    for first, last, order in splits:
        if last == first:
            continue
        cols = slice(first * HEAD_WIDTH, last * HEAD_WIDTH)
        for got, source in gather_order(jnp.concatenate([keys[:, cols], values[:, cols]], axis=1), order):
            key_rows = (source[:, None] * tok_dev + jnp.arange(tok_dev, dtype=jnp.int32)[None, :]).reshape(-1)
            gathered.append((got.reshape(key_rows.shape[0], -1), key_rows))
            bounds.append((first, last))
    late = [len(gathered) - 1 - k for k in range(len(gathered)) if k % 2 == 0]
    held, weight_rows = lax.optimization_barrier(([gathered[k] for k in late], weight_rows))
    for k, piece in zip(late, held):
        gathered[k] = piece
    numerators, denominators = [], []
    states = {}
    for (first, last), (got, key_rows) in zip(bounds, gathered):
        width = (last - first) * HEAD_WIDTH
        q_part = q_groups[:, first:last]
        state = states.get((first, last), (
            jnp.zeros((last - first, group_repeat, tok_dev, HEAD_WIDTH), jnp.float32),
            jnp.zeros((last - first, group_repeat, tok_dev), jnp.float32),
        ))
        states[(first, last)] = attend(state, q_part, got[:, :width], got[:, width:], key_rows)
    for key in sorted(states):
        numerators.append(states[key][0])
        denominators.append(states[key][1])
    numerator = jnp.concatenate(numerators, axis=0)
    denominator = jnp.concatenate(denominators, axis=0)
    attended = (numerator / denominator[..., None]).astype(jnp.bfloat16)
    attended = attended.transpose(2, 0, 1, 3).reshape(tok_dev, kv_local * group_repeat * HEAD_WIDTH)
    all_heads = ring_all_gather(attended, "head").transpose(1, 0, 2).reshape(tok_dev, -1)
    blocks = all_heads.reshape(tok_dev, outer, inner, rows_each).transpose(2, 0, 1, 3)
    regrouped = permute_all_to_all(blocks, INNER)
    regrouped = jnp.take(regrouped.reshape(inner * tok_dev, outer, rows_each), arrival, axis=1)
    partial = jnp.dot(regrouped[:, 0], weight_rows[0], preferred_element_type=jnp.float32)
    for t in range(1, outer):
        partial = partial + jnp.dot(regrouped[:, t], weight_rows[t], preferred_element_type=jnp.float32)
    by_dest = partial.reshape(2, 2, tok_dev, -1)
    cut = by_dest.shape[-1] // 2
    mixed = jnp.concatenate([
        swap_reduce_scatter(by_dest[..., :cut], "c2", "c1"),
        swap_reduce_scatter(by_dest[..., cut:].transpose(1, 0, 2, 3), "c1", "c2"),
    ], axis=-1)
    hidden = hidden_in.astype(jnp.float32)
    sums = lax.psum(
        jnp.stack([
            jnp.sum(mixed * mixed, axis=1),
            jnp.sum(hidden * reward_weight[None, :], axis=1),
            jnp.sum(mixed * (out_gain * reward_weight)[None, :], axis=1),
        ]),
        "head",
    )
    rms = jnp.sqrt(sums[0] / D + 1e-06)
    normed = mixed / rms[:, None]
    out32 = hidden + normed * out_gain[None, :]
    tok_reward = sums[1] + sums[2] / rms
    onehot = (query_doc[:, None] == jnp.arange(NDOC, dtype=jnp.int32)[None, :]).astype(jnp.float32)
    partial_sums = jnp.sum(onehot * tok_reward[:, None], axis=0)
    totals = butterfly_sum(partial_sums, CTX)
    rewards = totals / jnp.sqrt(doc_lengths.astype(jnp.float32))
    return (out32.astype(jnp.bfloat16), rewards)


def solution(mesh):
    n_ctx, n_head = mesh.devices.shape
    split = Mesh(mesh.devices.reshape(n_ctx // 4, 2, 2, n_head), CTX + ("head",))
    rows = P(CTX, "head")
    in_specs = (rows, rows, rows, rows, rows, P("head"), P("head"), P())
    out_specs = (rows, P())
    return jax.shard_map(shards, mesh=split, in_specs=in_specs, out_specs=out_specs, check_vma=False)
```
